512 devices in a mesh: seq: 64 (over z, y), head: 8 (over x, core).
Axes of the slice: x: 4, y: 4, z: 16, core: 2. Of those that a mesh axis runs over, the one named last changes fastest.
Arguments:
- tokens_in: bfloat16 [8192, 2048], P('seq', 'head'), may hold values from -40 to 40
- mixed_qkv: bfloat16 [8192, 8192], P('seq', 'head'), may hold values from -6 to 6
- conv_weight: bfloat16 [4, 8192], P(None, 'head'), may hold values from -3 to 3
- conv_cache: bfloat16 [3, 8192], P(None, 'head'), may hold values from -6 to 6
- gate_z: bfloat16 [8192, 4096], P('seq', 'head'), may hold values from -6 to 6
- beta_logit: float32 [32, 8192], P('head', 'seq'), may hold values from -10 to 2.5
- log_decay: float32 [32, 8192], P('head', 'seq'), may hold values from -0.8 to 0
- init_state: float32 [32, 128, 128], P('head'), may hold values from -0.18 to 0.18
- norm_weight: float32 [128], replicated, may hold values from 0.25 to 1.75
- out_weight: bfloat16 [4096, 2048], P('head'), may hold values from -0.09375 to 0.09375
- steer_table: float32 [16, 2048], P(None, 'head'), may hold values from -4.2 to 4.2
- steer_index: int32 [8192], P('seq'), may hold values from 0 to 15
- post_norm_weight: float32 [2048], P('head'), may hold values from 0.25 to 1.75
- route_ids: int32 [8192, 10], P('seq'), may hold values from 0 to 255, all different within a row; in each aligned block of 128 rows (0 to 127, 128 to 255, ...) at most 6 rows name the same one
- route_weight: float32 [8192, 10], P('seq'), may hold values from 0.1 to 1
- w_gate_up: bfloat16 [256, 2048, 512], P('seq', 'head'), may hold values from -0.125 to 0.125
- w_down: bfloat16 [256, 256, 2048], P('seq', None, 'head'), may hold values from -0.375 to 0.375
Outputs:
- layer_out: bfloat16 [8192, 2048], P('seq', 'head')
The draws below stay inside these ranges and needn't reach their ends.
Inputs may be any that keep to these rules, and one draw needn't show every extreme that they name: `route_ids`: each row names 10 different experts. Among the 128 rows of one device no expert is named more than 6 times, and in some devices' rows some expert is named exactly 6 times.
All inputs are finite; a program needn't handle non-finite values.
Results may differ from the reference program's by a relative error of at most 0.017.
Values may be sent and summed in bfloat16 or wider, within the bound.
No kernel may reach another device: no remote copies, remote signals or barrier semaphores. Data moves between devices by JAX's collectives and lax.ppermute only.
A program may use at most 128 MiB of HBM per device.

```python
import math
import jax
import jax.numpy as jnp
import numpy as np
from jax import lax

D = 2048
HK = 16
VALUE_HEAD_COUNT = 32
DK = 128
DV = 128
KCONV = 4
FF = 256
TOP = 10
NSTEER = 16
TOK_DEV = 128
WINDOW_TOKENS = 8192
EXPERTS = 256
CAP = 6
N_SEQ = 64
N_HEAD = 8


def slow_heads(key):
    share = 0.5
    return jax.random.uniform(jax.random.fold_in(key, 101), (VALUE_HEAD_COUNT, 1)) < share


def draw_log_decay(key, part):
    slow = slow_heads(key)
    partition_keys = jax.random.split(jax.random.fold_in(key, 202), 6)
    devices = WINDOW_TOKENS // TOK_DEV
    head_decay_speed = jnp.exp(jax.random.uniform(partition_keys[0], (VALUE_HEAD_COUNT, 1), minval=jnp.log(0.1), maxval=jnp.log(0.4))) / WINDOW_TOKENS
    machine_multiplier = jnp.exp(jax.random.uniform(partition_keys[1], (VALUE_HEAD_COUNT, devices), minval=-0.7, maxval=0.7))
    machine_multiplier = jnp.repeat(machine_multiplier, TOK_DEV, axis=1)
    jaggedness = jnp.exp(jax.random.uniform(partition_keys[2], (VALUE_HEAD_COUNT, WINDOW_TOKENS), minval=-0.7, maxval=0.7))
    fast_rate = jnp.exp(jax.random.uniform(partition_keys[3], (VALUE_HEAD_COUNT, WINDOW_TOKENS), minval=jnp.log(0.04), maxval=jnp.log(0.08)))
    locations = jax.random.randint(partition_keys[4], (2, 1), 0, WINDOW_TOKENS)
    spike_amount = jnp.any(jnp.arange(WINDOW_TOKENS)[None, :] == locations, axis=0)[None, :]
    spike_penalty = jnp.log(jax.random.uniform(partition_keys[5], (VALUE_HEAD_COUNT, WINDOW_TOKENS), minval=0.5, maxval=0.8))
    gradual_logarithm = -head_decay_speed * machine_multiplier * jaggedness + jnp.where(spike_amount, spike_penalty, 0.0)
    return jnp.where(slow, gradual_logarithm, -fast_rate).astype(jnp.float32)


def draw_beta_logit(key, part):
    slow = slow_heads(key)
    partition_keys = jax.random.split(jax.random.fold_in(key, 303), 2)
    slow_beta = jnp.exp(jax.random.uniform(partition_keys[0], (VALUE_HEAD_COUNT, WINDOW_TOKENS), minval=jnp.log(0.04), maxval=jnp.log(0.3))) * DK / WINDOW_TOKENS
    fast_beta = jax.random.uniform(partition_keys[1], (VALUE_HEAD_COUNT, WINDOW_TOKENS), minval=0.2, maxval=0.9)
    strength = jnp.where(slow, slow_beta, fast_beta)
    return (jnp.log(strength) - jnp.log1p(-strength)).astype(jnp.float32)


def draw_tokens_in(key, part):
    partition_keys = jax.random.split(jax.random.fold_in(key, 404), 3)
    columns = jnp.arange(D, dtype=jnp.float32) / D
    col_scale = jnp.exp(jnp.log(3.0) * columns) * 10.0 ** jax.random.uniform(partition_keys[1], (D,)) / 20.0
    base = jnp.clip(jax.random.normal(partition_keys[0], (WINDOW_TOKENS, D)), -6.0, 6.0)
    row_scale = 10.0 ** (jax.random.uniform(partition_keys[2], (WINDOW_TOKENS, 1)) - 0.5)
    drawn = base * row_scale * col_scale
    return drawn.astype(jnp.bfloat16)


def with_ends(result, rng, least, top_value):
    longest = result.shape.index(max(result.shape))
    spots = []
    for shift in (0, 1):
        where = [jax.random.randint(jax.random.fold_in(rng, axis), (), 0, length) for axis, length in enumerate(result.shape)]
        where[longest] = (where[longest] + shift) % result.shape[longest]
        spots.append(tuple(where))
    return result.at[spots[0]].set(least).at[spots[1]].set(top_value)


def steps_of(stream_key, extent, cuts, low, high):
    gain = 1.0
    for axis_at, parts in cuts:
        draws = jax.random.uniform(jax.random.fold_in(jax.random.fold_in(stream_key, 6), axis_at), (parts,), jnp.float32, low / len(cuts), high / len(cuts))
        gain = gain * jnp.repeat(jnp.exp(draws), extent[axis_at] // parts).reshape((-1,) + (1,) * (len(extent) - 1 - axis_at))
    return gain


def routed_block(key, own, number, rows, count, top, bound, slope):
    sequence = jax.random.permutation(key, count)
    crowded, usual = load_shares(count, rows * top, bound, slope, True), load_shares(count, rows * top, bound, slope, False)
    places = jnp.arange(count)

    def named(tallies, rotation):
        used = int((tallies > 0).sum())
        fixed = max(1, used // 4)
        shifted = fixed + (places - fixed + rotation * (used - fixed)) % max(1, count - fixed)
        return jnp.zeros((count,), jnp.int32).at[sequence[jnp.where(places < fixed, places, shifted)]].set(jnp.asarray(tallies, jnp.int32))

    tallies = jnp.where(number % 4 == 0, named(crowded, number // 4), named(usual, number - number // 4 - 1))
    mixed = jax.random.permutation(jax.random.fold_in(own, 3), count)
    donor, sink = mixed[0:count // 2 * 2:2], mixed[1:count // 2 * 2:2]
    margin = jnp.minimum(tallies[donor] - 1, bound - tallies[sink]) // 2
    margin = jnp.where((donor == sequence[0]) | (sink == sequence[0]) | (tallies[sink] == 0), 0, jnp.maximum(margin, 0))
    shifted = jax.random.randint(jax.random.fold_in(own, 4), (count // 2,), 0, 1 << 20) % (margin + 1)
    tallies = tallies.at[donor].add(-shifted).at[sink].add(shifted)
    members = jnp.searchsorted(jnp.cumsum(tallies), jnp.arange(rows * top), side="right").astype(jnp.int32)
    listing = members.reshape(top, rows).T
    listing = listing[jax.random.permutation(jax.random.fold_in(own, 1), rows)]
    rotation = jax.random.randint(jax.random.fold_in(own, 2), (rows, 1), 0, top)
    return jnp.take_along_axis(listing, (jnp.arange(top)[None, :] + rotation) % top, axis=1)


def load_shares(number_of, total, bound, lean, full):
    portions = [(1 << 20) // math.isqrt(grade ** lean) + 1 for grade in range(1, number_of + 1)]
    largest = bound if full else min(bound, max(-(-total // number_of), total * portions[0] // sum(portions)))
    least = 1 if total - largest >= number_of - 1 else 0
    given, surplus = [largest] + [least] * (number_of - 1), total - largest - least * (number_of - 1)
    while surplus > 0:
        movable = [i for i in range(1, number_of) if given[i] < largest] or [i for i in range(1, number_of) if given[i] < bound]
        mass, budget = sum([portions[i] for i in movable]), surplus
        for i in movable:
            extra = min(bound - given[i], max(1, budget * portions[i] // mass), surplus)
            given[i] = given[i] + extra
            surplus = surplus - extra
    return np.array(given)


def centred(own_key, extent, deviation, reach, pieces=(), kind=jnp.bfloat16):
    result = jax.random.normal(own_key, extent, jnp.float32) * deviation
    if len(pieces) > 0:
        result = steps_of(own_key, extent, pieces, -0.22, 0.18) * result
    return jnp.clip(result, min=-reach, max=reach).astype(kind)


def setup_inputs(seed: int = 0) -> dict:
    key_list = jax.random.split(jax.random.key(seed), 18)
    tokens_in = draw_tokens_in(jax.random.fold_in(key_list[17], 71), 0)
    mixed_qkv = centred(key_list[1], (WINDOW_TOKENS, HK * (2 * DK + (VALUE_HEAD_COUNT // HK) * DV)), 1.0, 6.0, ((0, 64), (1, 8)))
    conv_weight = centred(key_list[2], (KCONV, HK * (2 * DK + (VALUE_HEAD_COUNT // HK) * DV)), KCONV ** -0.5, 3.0, ((1, 8),))
    conv_cache = centred(key_list[3], (KCONV - 1, HK * (2 * DK + (VALUE_HEAD_COUNT // HK) * DV)), 1.0, 6.0, ((1, 8),))
    gate_z = centred(key_list[4], (WINDOW_TOKENS, VALUE_HEAD_COUNT * DV), 1.0, 6.0, ((0, 64), (1, 8)))
    beta_logit = draw_beta_logit(jax.random.fold_in(key_list[17], 71), 0)
    log_decay = draw_log_decay(jax.random.fold_in(key_list[17], 71), 0)
    init_state = centred(key_list[7], (VALUE_HEAD_COUNT, DK, DV), 0.03, 0.18, ((0, 8),), jnp.float32)
    norm_weight = jnp.clip(1.0 + 0.15 * jax.random.normal(key_list[8], (DV,), jnp.float32), 0.25, 1.75)
    out_weight = centred(key_list[9], (VALUE_HEAD_COUNT * DV, D), (VALUE_HEAD_COUNT * DV) ** -0.5, 0.09375, ((0, 8),))
    steer_table = centred(key_list[10], (NSTEER, D), 0.7, 4.2, ((1, 8),), jnp.float32)
    steer_index = with_ends(jax.random.randint(key_list[11], (WINDOW_TOKENS,), 0, NSTEER), jax.random.fold_in(key_list[11], 1), 0, NSTEER - 1).astype(jnp.int32)
    post_norm_weight = jnp.clip(1.0 + 0.15 * jax.random.normal(key_list[12], (D,), jnp.float32), 0.25, 1.75)
    route_ids_keys = jax.random.split(jax.random.fold_in(key_list[13], 1), WINDOW_TOKENS // TOK_DEV)
    route_ids_turns = jax.random.permutation(jax.random.fold_in(key_list[13], 3), WINDOW_TOKENS // TOK_DEV)
    route_ids = jax.vmap(lambda own, number: routed_block(jax.random.fold_in(key_list[13], 2), own, number, TOK_DEV, EXPERTS, TOP, CAP, 2))(route_ids_keys, route_ids_turns).reshape((WINDOW_TOKENS, TOP))
    route_weight = jnp.clip(jnp.exp(math.log(1.0) - 2.3025851 * jax.random.uniform(key_list[14], (WINDOW_TOKENS, TOP), jnp.float32) ** steps_of(key_list[14], (WINDOW_TOKENS, TOP), ((0, 64),), -0.2, 0.2)), 0.1, 1.0)
    w_gate_up = centred(key_list[15], (EXPERTS, D, 2 * FF), D ** -0.5, 0.125, ((0, 64), (1, 8)))
    w_down = centred(key_list[16], (EXPERTS, FF, D), FF ** -0.5, 0.375, ((0, 64), (2, 8)))
    return dict(tokens_in=tokens_in, mixed_qkv=mixed_qkv, conv_weight=conv_weight, conv_cache=conv_cache, gate_z=gate_z, beta_logit=beta_logit, log_decay=log_decay, init_state=init_state, norm_weight=norm_weight, out_weight=out_weight, steer_table=steer_table, steer_index=steer_index, post_norm_weight=post_norm_weight, route_ids=route_ids, route_weight=route_weight, w_gate_up=w_gate_up, w_down=w_down)


EPS = 1e-06
EXACT_ARITHMETIC = lax.Precision.HIGHEST

def unit_rows(vectors):
    return vectors / jnp.sqrt(lax.optimization_barrier(jnp.sum(vectors * vectors, axis=-1, keepdims=True)) + EPS)

def reference(tokens_in, mixed_qkv, conv_weight, conv_cache, gate_z, beta_logit, log_decay, init_state, norm_weight, out_weight, steer_table, steer_index, post_norm_weight, route_ids, route_weight, w_gate_up, w_down):
    padded = jnp.concatenate([conv_cache, mixed_qkv], axis=0).astype(jnp.float32)
    conv_taps = conv_weight.astype(jnp.float32)
    convolved = conv_taps[0] * padded[0:WINDOW_TOKENS]
    for offset in range(1, KCONV):
        convolved = convolved + conv_taps[offset] * padded[offset:offset + WINDOW_TOKENS]
    convolved = jax.nn.silu(convolved).reshape(WINDOW_TOKENS, HK, -1)
    queries = jnp.repeat(unit_rows(convolved[:, :, :DK]) * DK ** (-0.5), VALUE_HEAD_COUNT // HK, axis=1)
    key_rows = jnp.repeat(unit_rows(convolved[:, :, DK:2 * DK]), VALUE_HEAD_COUNT // HK, axis=1)
    values = convolved[:, :, 2 * DK:].reshape(WINDOW_TOKENS, VALUE_HEAD_COUNT, DV)
    beta_rate = jax.nn.sigmoid(beta_logit).T
    decay_rate = jnp.exp(log_decay).T

    def advance(current_state, inputs):
        query_vector, single_key_row, value, beta_now, decay_now = inputs
        current_state = current_state * decay_now[:, None, None]
        retrieved_value = jnp.einsum('qlp,ql->qp', current_state, single_key_row, precision=EXACT_ARITHMETIC)
        update = beta_now[:, None] * (value - retrieved_value)
        current_state = current_state + single_key_row[:, :, None] * update[:, None, :]
        return (current_state, jnp.einsum('qlp,ql->qp', current_state, query_vector, precision=EXACT_ARITHMETIC))
    unused_state, delta_out = lax.scan(advance, init_state, (queries, key_rows, values, beta_rate, decay_rate))
    inv_rms = lax.rsqrt(lax.optimization_barrier(jnp.mean(delta_out * delta_out, axis=-1, keepdims=True)) + EPS)
    gate_act = jax.nn.silu(gate_z.astype(jnp.float32)).reshape(WINDOW_TOKENS, VALUE_HEAD_COUNT, DV)
    normed_heads = (delta_out * inv_rms * norm_weight * gate_act).astype(jnp.bfloat16).reshape(WINDOW_TOKENS, VALUE_HEAD_COUNT * DV)
    group_rows = VALUE_HEAD_COUNT * DV // N_HEAD
    attended = jnp.zeros((WINDOW_TOKENS, D), jnp.float32)
    for group_index in range(N_HEAD):
        lower_row = group_index * group_rows
        partial_value = jnp.dot(normed_heads[:, lower_row:lower_row + group_rows], out_weight[lower_row:lower_row + group_rows], preferred_element_type=jnp.float32)
        attended = attended + lax.optimization_barrier(partial_value.astype(jnp.bfloat16)).astype(jnp.float32)
    hidden = tokens_in.astype(jnp.float32) + attended
    steered = hidden + steer_table[steer_index]
    sum_hidden = lax.optimization_barrier(jnp.sum(hidden * hidden, axis=1, keepdims=True))
    sum_steered = lax.optimization_barrier(jnp.sum(steered * steered, axis=1, keepdims=True))
    rescaled = steered * jnp.sqrt((sum_hidden / D + EPS) / (sum_steered / D + EPS))
    normed = (post_norm_weight * steered * lax.rsqrt(sum_steered / D + EPS)).astype(jnp.bfloat16)
    route_mix = route_weight / lax.optimization_barrier(jnp.sum(route_weight, axis=1, keepdims=True))
    flat_ids = route_ids.reshape(-1).astype(jnp.int32)
    total_rows = flat_ids.shape[0]
    order = jnp.argsort(flat_ids, stable=True).astype(jnp.int32)
    sorted_ids = flat_ids[order]
    counts = jnp.zeros((EXPERTS,), jnp.int32).at[flat_ids].add(1)
    starts = jnp.cumsum(counts) - counts
    sorted_rank = jnp.arange(total_rows, dtype=jnp.int32) - starts[sorted_ids]
    slot_rank = jnp.zeros((total_rows,), jnp.int32).at[order].set(sorted_rank)
    slot_span = N_SEQ * CAP
    slot_place = flat_ids * slot_span + slot_rank
    token_of = jnp.full((EXPERTS * slot_span,), WINDOW_TOKENS, jnp.int32).at[slot_place].set(jnp.arange(total_rows, dtype=jnp.int32) // TOP)
    weight_of = jnp.zeros((EXPERTS * slot_span,), jnp.float32).at[slot_place].set(route_mix.reshape(-1))
    padded_rows = jnp.concatenate([normed, jnp.zeros((1, D), jnp.bfloat16)], axis=0)
    feature_block = D // N_HEAD

    def expert_step(expert_mix, expert):
        first_slot = (expert * slot_span).astype(jnp.int32)
        tokens_here = lax.dynamic_slice_in_dim(token_of, first_slot, slot_span)
        weights_here = lax.dynamic_slice_in_dim(weight_of, first_slot, slot_span)
        rows_here = jnp.take(padded_rows, tokens_here, axis=0)
        gate_up = jnp.zeros((slot_span, 2 * FF), jnp.float32)
        for block_index in range(N_HEAD):
            lower_col = block_index * feature_block
            term_block = jnp.dot(rows_here[:, lower_col:lower_col + feature_block], w_gate_up[expert, lower_col:lower_col + feature_block], preferred_element_type=jnp.float32)
            gate_up = gate_up + lax.optimization_barrier(term_block.astype(jnp.bfloat16)).astype(jnp.float32)
        activated = (jax.nn.silu(gate_up[:, :FF]) * gate_up[:, FF:]).astype(jnp.bfloat16)
        produced = jnp.dot(activated, w_down[expert], preferred_element_type=jnp.float32).astype(jnp.bfloat16)
        expert_mix = expert_mix.at[tokens_here].add(weights_here[:, None] * produced.astype(jnp.float32))
        return (expert_mix, None)
    expert_mix, unused_rows = lax.scan(expert_step, jnp.zeros((WINDOW_TOKENS + 1, D), jnp.float32), jnp.arange(EXPERTS, dtype=jnp.int32))
    return (rescaled + expert_mix[:WINDOW_TOKENS]).astype(jnp.bfloat16)
```

```python
import functools

import jax
import jax.numpy as jnp
from jax import lax
from jax.sharding import PartitionSpec as P

D = 2048
HK = 16
VALUE_HEAD_COUNT = 32
DK = 128
DV = 128
KCONV = 4
STRETCH = 64


EPS = 1e-06
EXACT_ARITHMETIC = lax.Precision.HIGHEST


def passed_along(value, axis, steps):
    count = lax.axis_size(axis)
    first, last = (max(0, -steps), min(count, count - steps))
    return lax.ppermute(value, axis, [(source, source + steps) for source in range(first, last)])


def unit_rows(vectors):
    return vectors / jnp.sqrt(jnp.sum(vectors * vectors, axis=-1, keepdims=True) + EPS)


def delta_block(want_output, carry_state, block):
    query_block, key_block, value_block, beta_block, decay_block = block
    block_len = query_block.shape[1]
    cum_decay = jnp.cumsum(decay_block, axis=-1)
    positions = jnp.arange(block_len)
    lower_mask = positions[:, None] >= positions[None, :]
    strict = positions[:, None] > positions[None, :]
    decay_diff = cum_decay[:, :, None] - cum_decay[:, None, :]
    inner = jnp.where(lower_mask, jnp.exp(jnp.where(lower_mask, decay_diff, 0.0)), 0.0)
    keys_keys = jnp.einsum("hck,hdk->hcd", key_block, key_block, precision=EXACT_ARITHMETIC)
    system = jnp.eye(block_len, dtype=jnp.float32) + beta_block[:, :, None] * jnp.where(
        strict, inner * keys_keys, 0.0
    )
    growth = jnp.exp(cum_decay)
    known_part = jnp.einsum("hck,hkw->hcw", key_block, carry_state, precision=EXACT_ARITHMETIC)
    target = beta_block[:, :, None] * (value_block - growth[:, :, None] * known_part)
    update = lax.linalg.triangular_solve(
        system, target, left_side=True, lower=True, unit_diagonal=True
    )
    tail_decay = jnp.exp(cum_decay[:, -1:] - cum_decay)
    new_state = growth[:, -1][:, None, None] * carry_state + jnp.einsum(
        "hck,hcw->hkw", key_block * tail_decay[:, :, None], update, precision=EXACT_ARITHMETIC
    )
    if not want_output:
        return (new_state, None)
    query_keys = jnp.einsum("hck,hdk->hcd", query_block, key_block, precision=EXACT_ARITHMETIC)
    output = growth[:, :, None] * jnp.einsum(
        "hck,hkw->hcw", query_block, carry_state, precision=EXACT_ARITHMETIC
    )
    output = output + jnp.einsum(
        "hcd,hdw->hcw", inner * query_keys, update, precision=EXACT_ARITHMETIC
    )
    return (new_state, output)


def delta_pass(queries, key_rows, values, beta_rate, decays, state_start, want_output):
    value_heads, length = beta_rate.shape
    block_count = length // STRETCH

    def to_blocks(tensor):
        shaped = tensor.reshape((value_heads, block_count, STRETCH) + tensor.shape[2:])
        return jnp.moveaxis(shaped, 1, 0)

    state_end, outputs = lax.scan(
        functools.partial(delta_block, want_output),
        state_start,
        (
            to_blocks(queries),
            to_blocks(key_rows),
            to_blocks(values),
            to_blocks(beta_rate),
            to_blocks(decays),
        ),
    )
    if want_output:
        outputs = jnp.moveaxis(outputs, 0, 1).reshape(value_heads, length, -1)
    return (state_end, outputs)


def entering_state(transfer, carried, init_state):
    count, position = (lax.axis_size("seq"), lax.axis_index("seq"))
    first = position == 0
    folded = (
        jnp.einsum("hij,hjk->hik", transfer, init_state, precision=EXACT_ARITHMETIC) + carried
    )
    shift = jnp.where(first, folded, carried)
    mapping = jnp.where(first, jnp.zeros_like(transfer), transfer)
    step = 1
    while step < count:
        if 2 * step >= count:
            shift_in = passed_along(shift, "seq", step)
            shift = (
                jnp.einsum("hij,hjk->hik", mapping, shift_in, precision=EXACT_ARITHMETIC) + shift
            )
        else:
            both_in = passed_along(jnp.concatenate([mapping, shift], axis=2), "seq", step)
            map_in, shift_in = both_in[:, :, :DK], both_in[:, :, DK:]
            shift = (
                jnp.einsum("hij,hjk->hik", mapping, shift_in, precision=EXACT_ARITHMETIC) + shift
            )
            mapping = jnp.einsum("hij,hjk->hik", mapping, map_in, precision=EXACT_ARITHMETIC)
        step *= 2
    before = passed_along(shift, "seq", 1)
    return before + first.astype(jnp.float32) * init_state


def local(
    tokens_in,
    mixed_qkv,
    conv_weight,
    conv_cache,
    gate_z,
    beta_logit,
    log_decay,
    init_state,
    norm_weight,
    out_weight,
    steer_table,
    steer_index,
    post_norm_weight,
    route_ids,
    route_weight,
    w_gate_up,
    w_down,
):
    length, channels = mixed_qkv.shape
    value_heads = beta_logit.shape[0]
    group_width = 2 * DK + VALUE_HEAD_COUNT // HK * DV
    key_heads = channels // group_width
    group_size = value_heads // key_heads
    boundary_rows = passed_along(mixed_qkv[length - (KCONV - 1) :], "seq", 1)
    is_first = (lax.axis_index("seq") == 0).astype(jnp.float32)
    preceding = boundary_rows.astype(jnp.float32) + is_first * conv_cache.astype(jnp.float32)
    padded = jnp.concatenate([preceding, mixed_qkv.astype(jnp.float32)], axis=0)
    conv_taps = conv_weight.astype(jnp.float32)
    convolved = conv_taps[0] * padded[0:length]
    for offset in range(1, KCONV):
        convolved = convolved + conv_taps[offset] * padded[offset : offset + length]
    convolved = jax.nn.silu(convolved).reshape(length, key_heads, group_width)
    queries = jnp.repeat(unit_rows(convolved[:, :, :DK]) * DK ** (-0.5), group_size, axis=1)
    key_rows = jnp.repeat(unit_rows(convolved[:, :, DK : 2 * DK]), group_size, axis=1)
    values = convolved[:, :, 2 * DK :].reshape(length, value_heads, DV)
    queries = jnp.transpose(queries, (1, 0, 2))
    key_rows = jnp.transpose(key_rows, (1, 0, 2))
    values = jnp.transpose(values, (1, 0, 2))
    beta_rate = jax.nn.sigmoid(beta_logit)
    identity_maps = jnp.broadcast_to(jnp.eye(DK, dtype=jnp.float32), (value_heads, DK, DK))
    state_start = jnp.concatenate(
        [jnp.zeros((value_heads, DK, DV), jnp.float32), identity_maps], axis=2
    )
    wide_values = jnp.concatenate(
        [values, jnp.zeros((value_heads, length, DK), jnp.float32)], axis=2
    )
    state_end, wide_out = delta_pass(
        queries, key_rows, wide_values, beta_rate, log_decay, state_start, True
    )
    entering = entering_state(state_end[:, :, DV:], state_end[:, :, :DV], init_state)
    delta_out = wide_out[:, :, :DV] + jnp.einsum(
        "hlk,hkv->hlv", wide_out[:, :, DV:], entering, precision=EXACT_ARITHMETIC
    )
    delta_out = jnp.transpose(delta_out, (1, 0, 2))
    inv_rms = lax.rsqrt(jnp.mean(delta_out * delta_out, axis=-1, keepdims=True) + EPS)
    gate_act = jax.nn.silu(gate_z.astype(jnp.float32)).reshape(length, value_heads, DV)
    normed_heads = (
        (delta_out * inv_rms * norm_weight * gate_act)
        .astype(jnp.bfloat16)
        .reshape(length, value_heads * DV)
    )
    partial_value = jnp.dot(normed_heads, out_weight, preferred_element_type=jnp.float32)
    attended = lax.psum_scatter(
        partial_value.astype(jnp.bfloat16), "head", scatter_dimension=1, tiled=True
    ).astype(jnp.float32)
    hidden = tokens_in.astype(jnp.float32) + attended
    steer_onehot = (steer_index[:, None] == jnp.arange(steer_table.shape[0])[None, :]).astype(
        jnp.float32
    )
    steered = hidden + jnp.dot(
        steer_onehot, steer_table, precision=EXACT_ARITHMETIC, preferred_element_type=jnp.float32
    )
    sum_hidden, sum_steered = lax.psum(
        (jnp.sum(hidden * hidden, axis=1), jnp.sum(steered * steered, axis=1)), "head"
    )
    rescaled = steered * jnp.sqrt((sum_hidden / D + EPS) / (sum_steered / D + EPS))[:, None]
    normed = (post_norm_weight * steered * lax.rsqrt(sum_steered / D + EPS)[:, None]).astype(
        jnp.bfloat16
    )
    experts_here = w_gate_up.shape[0]
    seq_size = lax.axis_size("seq")
    experts = experts_here * seq_size
    top_count = route_ids.shape[1]
    capacity = 5 * length * top_count // (4 * experts)
    slot_count = seq_size * capacity * experts_here
    flat_ids = route_ids.reshape(-1)
    expert_hits = (flat_ids[:, None] == jnp.arange(experts, dtype=jnp.int32)[None, :]).astype(
        jnp.int32
    )
    slot_rank = jnp.sum(jnp.cumsum(expert_hits, axis=0) * expert_hits, axis=1) - 1
    owner_dev = flat_ids // experts_here
    local_expert = flat_ids % experts_here
    slot_place = (owner_dev * capacity + slot_rank) * experts_here + local_expert
    source = (
        jnp.full((slot_count,), length, jnp.int32)
        .at[slot_place]
        .set(jnp.arange(flat_ids.shape[0], dtype=jnp.int32) // top_count)
    )
    padded_rows = jnp.concatenate([normed, jnp.zeros((1, normed.shape[1]), jnp.bfloat16)], axis=0)
    outgoing = jnp.take(padded_rows, source, axis=0).reshape(seq_size, capacity, experts_here, -1)
    arrived = lax.all_to_all(outgoing, "seq", split_axis=0, concat_axis=0, tiled=True)
    row_count = seq_size * capacity
    arrived = arrived.reshape(row_count, experts_here, -1)
    ffn_width = w_down.shape[1]
    term_rows = jnp.einsum("red,edf->ref", arrived, w_gate_up, preferred_element_type=jnp.float32)
    summed = lax.psum(term_rows.reshape(row_count, -1).astype(jnp.bfloat16), "head").astype(
        jnp.float32
    )
    activate_summed = summed
    activate_summed = activate_summed.reshape(activate_summed.shape[0], experts_here, 2 * ffn_width)
    results = jnp.einsum(
        "ref,efd->red",
        (jax.nn.silu(activate_summed[:, :, :ffn_width]) * activate_summed[:, :, ffn_width:]).astype(
            jnp.bfloat16
        ),
        w_down,
        preferred_element_type=jnp.float32,
    ).astype(jnp.bfloat16)
    returned = lax.all_to_all(
        results.reshape(seq_size, capacity, experts_here, -1),
        "seq",
        split_axis=0,
        concat_axis=0,
        tiled=True,
    )
    returned = returned.reshape(slot_count, -1)
    route_mix = route_weight / jnp.sum(route_weight, axis=1, keepdims=True)
    picked = jnp.take(returned, slot_place, axis=0).reshape(length, top_count, -1)
    expert_mix = jnp.sum(picked.astype(jnp.float32) * route_mix[:, :, None], axis=1)
    return (rescaled + expert_mix).astype(jnp.bfloat16)


def solution(mesh):
    placed = (
        P("seq", "head"),
        P("seq", "head"),
        P(None, "head"),
        P(None, "head"),
        P("seq", "head"),
        P("head", "seq"),
        P("head", "seq"),
        P("head", None, None),
        P(),
        P("head", None),
        P(None, "head"),
        P("seq"),
        P("head"),
        P("seq", None),
        P("seq", None),
        P("seq", "head", None),
        P("seq", None, "head"),
    )
    return jax.shard_map(
        local, mesh=mesh, in_specs=placed, out_specs=P("seq", "head"), check_vma=False
    )
```

```python
import functools

import jax
import jax.numpy as jnp
from jax import lax
from jax.sharding import PartitionSpec as P

D = 2048
HK = 16
VALUE_HEAD_COUNT = 32
DK = 128
DV = 128
KCONV = 4
STRETCH = 64


EPS = 1e-06
EXACT_ARITHMETIC = lax.Precision.HIGHEST


def passed_along(value, axis, steps):
    count = lax.axis_size(axis)
    first, last = (max(0, -steps), min(count, count - steps))
    return lax.ppermute(value, axis, [(source, source + steps) for source in range(first, last)])


def unit_rows(vectors):
    return vectors / jnp.sqrt(jnp.sum(vectors * vectors, axis=-1, keepdims=True) + EPS)


def delta_block(want_output, carry_state, block):
    query_block, key_block, value_block, beta_block, decay_block = block
    block_len = query_block.shape[1]
    cum_decay = jnp.cumsum(decay_block, axis=-1)
    positions = jnp.arange(block_len)
    lower_mask = positions[:, None] >= positions[None, :]
    strict = positions[:, None] > positions[None, :]
    decay_diff = cum_decay[:, :, None] - cum_decay[:, None, :]
    inner = jnp.where(lower_mask, jnp.exp(jnp.where(lower_mask, decay_diff, 0.0)), 0.0)
    keys_keys = jnp.einsum("hck,hdk->hcd", key_block, key_block, precision=EXACT_ARITHMETIC)
    system = jnp.eye(block_len, dtype=jnp.float32) + beta_block[:, :, None] * jnp.where(
        strict, inner * keys_keys, 0.0
    )
    growth = jnp.exp(cum_decay)
    known_part = jnp.einsum("hck,hkw->hcw", key_block, carry_state, precision=EXACT_ARITHMETIC)
    target = beta_block[:, :, None] * (value_block - growth[:, :, None] * known_part)
    update = lax.linalg.triangular_solve(
        system, target, left_side=True, lower=True, unit_diagonal=True
    )
    tail_decay = jnp.exp(cum_decay[:, -1:] - cum_decay)
    new_state = growth[:, -1][:, None, None] * carry_state + jnp.einsum(
        "hck,hcw->hkw", key_block * tail_decay[:, :, None], update, precision=EXACT_ARITHMETIC
    )
    if not want_output:
        return (new_state, None)
    query_keys = jnp.einsum("hck,hdk->hcd", query_block, key_block, precision=EXACT_ARITHMETIC)
    output = growth[:, :, None] * jnp.einsum(
        "hck,hkw->hcw", query_block, carry_state, precision=EXACT_ARITHMETIC
    )
    output = output + jnp.einsum(
        "hcd,hdw->hcw", inner * query_keys, update, precision=EXACT_ARITHMETIC
    )
    return (new_state, output)


def delta_pass(queries, key_rows, values, beta_rate, decays, state_start, want_output):
    value_heads, length = beta_rate.shape
    block_count = length // STRETCH

    def to_blocks(tensor):
        shaped = tensor.reshape((value_heads, block_count, STRETCH) + tensor.shape[2:])
        return jnp.moveaxis(shaped, 1, 0)

    state_end, outputs = lax.scan(
        functools.partial(delta_block, want_output),
        state_start,
        (
            to_blocks(queries),
            to_blocks(key_rows),
            to_blocks(values),
            to_blocks(beta_rate),
            to_blocks(decays),
        ),
    )
    if want_output:
        outputs = jnp.moveaxis(outputs, 0, 1).reshape(value_heads, length, -1)
    return (state_end, outputs)


SCAN_RADIX = 4


def compose(later, earlier):
    joined = jnp.einsum("hij,hjk->hik", later[:, :, :DK], earlier, precision=EXACT_ARITHMETIC)
    return joined + jnp.concatenate([jnp.zeros_like(later[:, :, :DK]), later[:, :, DK:]], axis=2)


def entering_state(transfer, carried, init_state):
    count, position = (lax.axis_size("seq"), lax.axis_index("seq"))
    first = position == 0
    folded = (
        jnp.einsum("hij,hjk->hik", transfer, init_state, precision=EXACT_ARITHMETIC) + carried
    )
    own = jnp.concatenate(
        [
            jnp.where(first, jnp.zeros_like(transfer), transfer),
            jnp.where(first, folded, carried),
        ],
        axis=2,
    )
    inclusive = own
    exclusive = None
    span = 1
    while span < count:
        for j in range(1, SCAN_RADIX):
            if span * j < count:
                part = passed_along(inclusive, "seq", span * j)
                exclusive = part if exclusive is None else compose(exclusive, part)
        span *= SCAN_RADIX
        if span < count:
            inclusive = compose(own, exclusive)
    return jnp.where(first, init_state, exclusive[:, :, DK:])


def local(
    tokens_in,
    mixed_qkv,
    conv_weight,
    conv_cache,
    gate_z,
    beta_logit,
    log_decay,
    init_state,
    norm_weight,
    out_weight,
    steer_table,
    steer_index,
    post_norm_weight,
    route_ids,
    route_weight,
    w_gate_up,
    w_down,
):
    length, channels = mixed_qkv.shape
    value_heads = beta_logit.shape[0]
    group_width = 2 * DK + VALUE_HEAD_COUNT // HK * DV
    key_heads = channels // group_width
    group_size = value_heads // key_heads
    boundary_rows = passed_along(mixed_qkv[length - (KCONV - 1) :], "seq", 1)
    is_first = (lax.axis_index("seq") == 0).astype(jnp.float32)
    preceding = boundary_rows.astype(jnp.float32) + is_first * conv_cache.astype(jnp.float32)
    padded = jnp.concatenate([preceding, mixed_qkv.astype(jnp.float32)], axis=0)
    conv_taps = conv_weight.astype(jnp.float32)
    convolved = conv_taps[0] * padded[0:length]
    for offset in range(1, KCONV):
        convolved = convolved + conv_taps[offset] * padded[offset : offset + length]
    convolved = jax.nn.silu(convolved).reshape(length, key_heads, group_width)
    queries = jnp.repeat(unit_rows(convolved[:, :, :DK]) * DK ** (-0.5), group_size, axis=1)
    key_rows = jnp.repeat(unit_rows(convolved[:, :, DK : 2 * DK]), group_size, axis=1)
    values = convolved[:, :, 2 * DK :].reshape(length, value_heads, DV)
    queries = jnp.transpose(queries, (1, 0, 2))
    key_rows = jnp.transpose(key_rows, (1, 0, 2))
    values = jnp.transpose(values, (1, 0, 2))
    beta_rate = jax.nn.sigmoid(beta_logit)
    identity_maps = jnp.broadcast_to(jnp.eye(DK, dtype=jnp.float32), (value_heads, DK, DK))
    state_start = jnp.concatenate(
        [jnp.zeros((value_heads, DK, DV), jnp.float32), identity_maps], axis=2
    )
    wide_values = jnp.concatenate(
        [values, jnp.zeros((value_heads, length, DK), jnp.float32)], axis=2
    )
    state_end, wide_out = delta_pass(
        queries, key_rows, wide_values, beta_rate, log_decay, state_start, True
    )
    entering = entering_state(state_end[:, :, DV:], state_end[:, :, :DV], init_state)
    delta_out = wide_out[:, :, :DV] + jnp.einsum(
        "hlk,hkv->hlv", wide_out[:, :, DV:], entering, precision=EXACT_ARITHMETIC
    )
    delta_out = jnp.transpose(delta_out, (1, 0, 2))
    inv_rms = lax.rsqrt(jnp.mean(delta_out * delta_out, axis=-1, keepdims=True) + EPS)
    gate_act = jax.nn.silu(gate_z.astype(jnp.float32)).reshape(length, value_heads, DV)
    normed_heads = (
        (delta_out * inv_rms * norm_weight * gate_act)
        .astype(jnp.bfloat16)
        .reshape(length, value_heads * DV)
    )
    partial_value = jnp.dot(normed_heads, out_weight, preferred_element_type=jnp.float32)
    attended = lax.psum_scatter(
        partial_value.astype(jnp.bfloat16), "head", scatter_dimension=1, tiled=True
    ).astype(jnp.float32)
    hidden = tokens_in.astype(jnp.float32) + attended
    steer_onehot = (steer_index[:, None] == jnp.arange(steer_table.shape[0])[None, :]).astype(
        jnp.float32
    )
    steered = hidden + jnp.dot(
        steer_onehot, steer_table, precision=EXACT_ARITHMETIC, preferred_element_type=jnp.float32
    )
    sum_hidden, sum_steered = lax.psum(
        (jnp.sum(hidden * hidden, axis=1), jnp.sum(steered * steered, axis=1)), "head"
    )
    rescaled = steered * jnp.sqrt((sum_hidden / D + EPS) / (sum_steered / D + EPS))[:, None]
    normed = (post_norm_weight * steered * lax.rsqrt(sum_steered / D + EPS)[:, None]).astype(
        jnp.bfloat16
    )
    experts_here = w_gate_up.shape[0]
    seq_size = lax.axis_size("seq")
    experts = experts_here * seq_size
    top_count = route_ids.shape[1]
    capacity = 5 * length * top_count // (4 * experts)
    slot_count = seq_size * capacity * experts_here
    flat_ids = route_ids.reshape(-1)
    expert_hits = (flat_ids[:, None] == jnp.arange(experts, dtype=jnp.int32)[None, :]).astype(
        jnp.int32
    )
    slot_rank = jnp.sum(jnp.cumsum(expert_hits, axis=0) * expert_hits, axis=1) - 1
    owner_dev = flat_ids // experts_here
    local_expert = flat_ids % experts_here
    slot_place = (owner_dev * capacity + slot_rank) * experts_here + local_expert
    source = (
        jnp.full((slot_count,), length, jnp.int32)
        .at[slot_place]
        .set(jnp.arange(flat_ids.shape[0], dtype=jnp.int32) // top_count)
    )
    padded_rows = jnp.concatenate([normed, jnp.zeros((1, normed.shape[1]), jnp.bfloat16)], axis=0)
    outgoing = jnp.take(padded_rows, source, axis=0).reshape(seq_size, capacity, experts_here, -1)
    arrived = lax.all_to_all(outgoing, "seq", split_axis=0, concat_axis=0, tiled=True)
    row_count = seq_size * capacity
    arrived = arrived.reshape(row_count, experts_here, -1)
    ffn_width = w_down.shape[1]
    term_rows = jnp.einsum("red,edf->ref", arrived, w_gate_up, preferred_element_type=jnp.float32)
    summed = lax.psum(term_rows.reshape(row_count, -1).astype(jnp.bfloat16), "head").astype(
        jnp.float32
    )
    activate_summed = summed
    activate_summed = activate_summed.reshape(activate_summed.shape[0], experts_here, 2 * ffn_width)
    results = jnp.einsum(
        "ref,efd->red",
        (jax.nn.silu(activate_summed[:, :, :ffn_width]) * activate_summed[:, :, ffn_width:]).astype(
            jnp.bfloat16
        ),
        w_down,
        preferred_element_type=jnp.float32,
    ).astype(jnp.bfloat16)
    returned = lax.all_to_all(
        results.reshape(seq_size, capacity, experts_here, -1),
        "seq",
        split_axis=0,
        concat_axis=0,
        tiled=True,
    )
    returned = returned.reshape(slot_count, -1)
    route_mix = route_weight / jnp.sum(route_weight, axis=1, keepdims=True)
    picked = jnp.take(returned, slot_place, axis=0).reshape(length, top_count, -1)
    expert_mix = jnp.sum(picked.astype(jnp.float32) * route_mix[:, :, None], axis=1)
    return (rescaled + expert_mix).astype(jnp.bfloat16)


def solution(mesh):
    placed = (
        P("seq", "head"),
        P("seq", "head"),
        P(None, "head"),
        P(None, "head"),
        P("seq", "head"),
        P("head", "seq"),
        P("head", "seq"),
        P("head", None, None),
        P(),
        P("head", None),
        P(None, "head"),
        P("seq"),
        P("head"),
        P("seq", None),
        P("seq", None),
        P("seq", "head", None),
        P("seq", None, "head"),
    )
    return jax.shard_map(
        local, mesh=mesh, in_specs=placed, out_specs=P("seq", "head"), check_vma=False
    )
```

```python
import functools

import jax
import jax.numpy as jnp
from jax import lax
from jax.sharding import PartitionSpec as P

D = 2048
HK = 16
VALUE_HEAD_COUNT = 32
DK = 128
DV = 128
KCONV = 4
STRETCH = 64


EPS = 1e-06
EXACT_ARITHMETIC = lax.Precision.HIGHEST


def passed_along(value, axis, steps):
    count = lax.axis_size(axis)
    first, last = (max(0, -steps), min(count, count - steps))
    return lax.ppermute(value, axis, [(source, source + steps) for source in range(first, last)])


def unit_rows(vectors):
    return vectors / jnp.sqrt(jnp.sum(vectors * vectors, axis=-1, keepdims=True) + EPS)


def delta_block(want_output, carry_state, block):
    query_block, key_block, value_block, beta_block, decay_block = block
    block_len = query_block.shape[1]
    cum_decay = jnp.cumsum(decay_block, axis=-1)
    positions = jnp.arange(block_len)
    lower_mask = positions[:, None] >= positions[None, :]
    strict = positions[:, None] > positions[None, :]
    decay_diff = cum_decay[:, :, None] - cum_decay[:, None, :]
    inner = jnp.where(lower_mask, jnp.exp(jnp.where(lower_mask, decay_diff, 0.0)), 0.0)
    keys_keys = jnp.einsum("hck,hdk->hcd", key_block, key_block, precision=EXACT_ARITHMETIC)
    system = jnp.eye(block_len, dtype=jnp.float32) + beta_block[:, :, None] * jnp.where(
        strict, inner * keys_keys, 0.0
    )
    growth = jnp.exp(cum_decay)
    known_part = jnp.einsum("hck,hkw->hcw", key_block, carry_state, precision=EXACT_ARITHMETIC)
    target = beta_block[:, :, None] * (value_block - growth[:, :, None] * known_part)
    update = lax.linalg.triangular_solve(
        system, target, left_side=True, lower=True, unit_diagonal=True
    )
    tail_decay = jnp.exp(cum_decay[:, -1:] - cum_decay)
    new_state = growth[:, -1][:, None, None] * carry_state + jnp.einsum(
        "hck,hcw->hkw", key_block * tail_decay[:, :, None], update, precision=EXACT_ARITHMETIC
    )
    if not want_output:
        return (new_state, None)
    query_keys = jnp.einsum("hck,hdk->hcd", query_block, key_block, precision=EXACT_ARITHMETIC)
    output = growth[:, :, None] * jnp.einsum(
        "hck,hkw->hcw", query_block, carry_state, precision=EXACT_ARITHMETIC
    )
    output = output + jnp.einsum(
        "hcd,hdw->hcw", inner * query_keys, update, precision=EXACT_ARITHMETIC
    )
    return (new_state, output)


def delta_pass(queries, key_rows, values, beta_rate, decays, state_start, want_output):
    value_heads, length = beta_rate.shape
    block_count = length // STRETCH

    def to_blocks(tensor):
        shaped = tensor.reshape((value_heads, block_count, STRETCH) + tensor.shape[2:])
        return jnp.moveaxis(shaped, 1, 0)

    state_end, outputs = lax.scan(
        functools.partial(delta_block, want_output),
        state_start,
        (
            to_blocks(queries),
            to_blocks(key_rows),
            to_blocks(values),
            to_blocks(beta_rate),
            to_blocks(decays),
        ),
    )
    if want_output:
        outputs = jnp.moveaxis(outputs, 0, 1).reshape(value_heads, length, -1)
    return (state_end, outputs)


def compose(later, earlier):
    joined = jnp.einsum("...ij,...jk->...ik", later[..., :DK], earlier, precision=EXACT_ARITHMETIC)
    return joined + jnp.concatenate([jnp.zeros_like(later[..., :DK]), later[..., DK:]], axis=-1)


def within_group(value, group, offset):
    count = lax.axis_size("seq")
    pairs = [
        (start + place, start + (place + offset) % group)
        for start in range(0, count, group)
        for place in range(group)
    ]
    return lax.ppermute(value, "seq", pairs)


def entering_state(transfer, carried, init_state):
    count, position = (lax.axis_size("seq"), lax.axis_index("seq"))
    group = transfer.shape[0]
    place = position % group
    first = position == 0
    folded = (
        jnp.einsum("hij,hjk->hik", transfer, init_state, precision=EXACT_ARITHMETIC) + carried
    )
    own = jnp.concatenate(
        [
            jnp.where(first, jnp.zeros_like(transfer), transfer),
            jnp.where(first, folded, carried),
        ],
        axis=2,
    )
    items = [lax.dynamic_index_in_dim(own, place, 0, keepdims=False)]
    for offset in range(1, group):
        sent = lax.dynamic_index_in_dim(own, (place + offset) % group, 0, keepdims=False)
        items.append(within_group(sent, group, offset))
    stacked = jnp.stack(items)
    maps = jnp.take(stacked, (place - jnp.arange(group)) % group, axis=0)
    identity = jnp.concatenate(
        [jnp.eye(DK, dtype=jnp.float32), jnp.zeros((DK, DV), jnp.float32)], axis=1
    )
    prefixes = [identity]
    for member in range(group):
        prefixes.append(compose(maps[member], prefixes[-1]) if member else maps[0])
    total = prefixes.pop()
    groups = count // group
    mapping, shift = total[:, :DK], total[:, DK:]
    step = 1
    while step < groups:
        if 2 * step >= groups:
            shift_in = passed_along(shift, "seq", step * group)
            shift = jnp.dot(mapping, shift_in, precision=EXACT_ARITHMETIC) + shift
        else:
            both_in = passed_along(jnp.concatenate([mapping, shift], axis=1), "seq", step * group)
            map_in, shift_in = both_in[:, :DK], both_in[:, DK:]
            shift = jnp.dot(mapping, shift_in, precision=EXACT_ARITHMETIC) + shift
            mapping = jnp.dot(mapping, map_in, precision=EXACT_ARITHMETIC)
        step *= 2
    start_state = passed_along(shift, "seq", group) + (position < group).astype(
        jnp.float32
    ) * lax.dynamic_index_in_dim(init_state, place, 0, keepdims=False)
    prefixes = jnp.stack(prefixes)
    entering = (
        jnp.einsum("pij,jk->pik", prefixes[:, :, :DK], start_state, precision=EXACT_ARITHMETIC)
        + prefixes[:, :, DK:]
    )
    heads = [lax.dynamic_index_in_dim(entering, place, 0, keepdims=False)]
    for offset in range(1, group):
        sent = lax.dynamic_index_in_dim(entering, (place + offset) % group, 0, keepdims=False)
        heads.append(within_group(sent, group, offset))
    stacked = jnp.stack(heads)
    return jnp.take(stacked, (place - jnp.arange(group)) % group, axis=0)


def local(
    tokens_in,
    mixed_qkv,
    conv_weight,
    conv_cache,
    gate_z,
    beta_logit,
    log_decay,
    init_state,
    norm_weight,
    out_weight,
    steer_table,
    steer_index,
    post_norm_weight,
    route_ids,
    route_weight,
    w_gate_up,
    w_down,
):
    length, channels = mixed_qkv.shape
    value_heads = beta_logit.shape[0]
    group_width = 2 * DK + VALUE_HEAD_COUNT // HK * DV
    key_heads = channels // group_width
    group_size = value_heads // key_heads
    boundary_rows = passed_along(mixed_qkv[length - (KCONV - 1) :], "seq", 1)
    is_first = (lax.axis_index("seq") == 0).astype(jnp.float32)
    preceding = boundary_rows.astype(jnp.float32) + is_first * conv_cache.astype(jnp.float32)
    padded = jnp.concatenate([preceding, mixed_qkv.astype(jnp.float32)], axis=0)
    conv_taps = conv_weight.astype(jnp.float32)
    convolved = conv_taps[0] * padded[0:length]
    for offset in range(1, KCONV):
        convolved = convolved + conv_taps[offset] * padded[offset : offset + length]
    convolved = jax.nn.silu(convolved).reshape(length, key_heads, group_width)
    queries = jnp.repeat(unit_rows(convolved[:, :, :DK]) * DK ** (-0.5), group_size, axis=1)
    key_rows = jnp.repeat(unit_rows(convolved[:, :, DK : 2 * DK]), group_size, axis=1)
    values = convolved[:, :, 2 * DK :].reshape(length, value_heads, DV)
    queries = jnp.transpose(queries, (1, 0, 2))
    key_rows = jnp.transpose(key_rows, (1, 0, 2))
    values = jnp.transpose(values, (1, 0, 2))
    beta_rate = jax.nn.sigmoid(beta_logit)
    identity_maps = jnp.broadcast_to(jnp.eye(DK, dtype=jnp.float32), (value_heads, DK, DK))
    state_start = jnp.concatenate(
        [jnp.zeros((value_heads, DK, DV), jnp.float32), identity_maps], axis=2
    )
    wide_values = jnp.concatenate(
        [values, jnp.zeros((value_heads, length, DK), jnp.float32)], axis=2
    )
    state_end, wide_out = delta_pass(
        queries, key_rows, wide_values, beta_rate, log_decay, state_start, True
    )
    entering = entering_state(state_end[:, :, DV:], state_end[:, :, :DV], init_state)
    delta_out = wide_out[:, :, :DV] + jnp.einsum(
        "hlk,hkv->hlv", wide_out[:, :, DV:], entering, precision=EXACT_ARITHMETIC
    )
    delta_out = jnp.transpose(delta_out, (1, 0, 2))
    inv_rms = lax.rsqrt(jnp.mean(delta_out * delta_out, axis=-1, keepdims=True) + EPS)
    gate_act = jax.nn.silu(gate_z.astype(jnp.float32)).reshape(length, value_heads, DV)
    normed_heads = (
        (delta_out * inv_rms * norm_weight * gate_act)
        .astype(jnp.bfloat16)
        .reshape(length, value_heads * DV)
    )
    partial_value = jnp.dot(normed_heads, out_weight, preferred_element_type=jnp.float32)
    attended = lax.psum_scatter(
        partial_value.astype(jnp.bfloat16), "head", scatter_dimension=1, tiled=True
    ).astype(jnp.float32)
    hidden = tokens_in.astype(jnp.float32) + attended
    steer_onehot = (steer_index[:, None] == jnp.arange(steer_table.shape[0])[None, :]).astype(
        jnp.float32
    )
    steered = hidden + jnp.dot(
        steer_onehot, steer_table, precision=EXACT_ARITHMETIC, preferred_element_type=jnp.float32
    )
    sum_hidden, sum_steered = lax.psum(
        (jnp.sum(hidden * hidden, axis=1), jnp.sum(steered * steered, axis=1)), "head"
    )
    rescaled = steered * jnp.sqrt((sum_hidden / D + EPS) / (sum_steered / D + EPS))[:, None]
    normed = (post_norm_weight * steered * lax.rsqrt(sum_steered / D + EPS)[:, None]).astype(
        jnp.bfloat16
    )
    experts_here = w_gate_up.shape[0]
    seq_size = lax.axis_size("seq")
    experts = experts_here * seq_size
    top_count = route_ids.shape[1]
    capacity = 5 * length * top_count // (4 * experts)
    slot_count = seq_size * capacity * experts_here
    flat_ids = route_ids.reshape(-1)
    expert_hits = (flat_ids[:, None] == jnp.arange(experts, dtype=jnp.int32)[None, :]).astype(
        jnp.int32
    )
    slot_rank = jnp.sum(jnp.cumsum(expert_hits, axis=0) * expert_hits, axis=1) - 1
    owner_dev = flat_ids // experts_here
    local_expert = flat_ids % experts_here
    slot_place = (owner_dev * capacity + slot_rank) * experts_here + local_expert
    source = (
        jnp.full((slot_count,), length, jnp.int32)
        .at[slot_place]
        .set(jnp.arange(flat_ids.shape[0], dtype=jnp.int32) // top_count)
    )
    padded_rows = jnp.concatenate([normed, jnp.zeros((1, normed.shape[1]), jnp.bfloat16)], axis=0)
    outgoing = jnp.take(padded_rows, source, axis=0).reshape(seq_size, capacity, experts_here, -1)
    arrived = lax.all_to_all(outgoing, "seq", split_axis=0, concat_axis=0, tiled=True)
    row_count = seq_size * capacity
    arrived = arrived.reshape(row_count, experts_here, -1)
    ffn_width = w_down.shape[1]
    term_rows = jnp.einsum("red,edf->ref", arrived, w_gate_up, preferred_element_type=jnp.float32)
    summed = lax.psum(term_rows.reshape(row_count, -1).astype(jnp.bfloat16), "head").astype(
        jnp.float32
    )
    activate_summed = summed
    activate_summed = activate_summed.reshape(activate_summed.shape[0], experts_here, 2 * ffn_width)
    results = jnp.einsum(
        "ref,efd->red",
        (jax.nn.silu(activate_summed[:, :, :ffn_width]) * activate_summed[:, :, ffn_width:]).astype(
            jnp.bfloat16
        ),
        w_down,
        preferred_element_type=jnp.float32,
    ).astype(jnp.bfloat16)
    returned = lax.all_to_all(
        results.reshape(seq_size, capacity, experts_here, -1),
        "seq",
        split_axis=0,
        concat_axis=0,
        tiled=True,
    )
    returned = returned.reshape(slot_count, -1)
    route_mix = route_weight / jnp.sum(route_weight, axis=1, keepdims=True)
    picked = jnp.take(returned, slot_place, axis=0).reshape(length, top_count, -1)
    expert_mix = jnp.sum(picked.astype(jnp.float32) * route_mix[:, :, None], axis=1)
    return (rescaled + expert_mix).astype(jnp.bfloat16)


def solution(mesh):
    placed = (
        P("seq", "head"),
        P("seq", "head"),
        P(None, "head"),
        P(None, "head"),
        P("seq", "head"),
        P("head", "seq"),
        P("head", "seq"),
        P("head", None, None),
        P(),
        P("head", None),
        P(None, "head"),
        P("seq"),
        P("head"),
        P("seq", None),
        P("seq", None),
        P("seq", "head", None),
        P("seq", None, "head"),
    )
    return jax.shard_map(
        local, mesh=mesh, in_specs=placed, out_specs=P("seq", "head"), check_vma=False
    )
```

```python
import functools

import jax
import jax.numpy as jnp
from jax import lax
from jax.sharding import PartitionSpec as P

D = 2048
HK = 16
VALUE_HEAD_COUNT = 32
DK = 128
DV = 128
KCONV = 4
STRETCH = 128


EPS = 1e-06
EXACT_ARITHMETIC = lax.Precision.HIGHEST


def passed_along(value, axis, steps):
    count = lax.axis_size(axis)
    first, last = (max(0, -steps), min(count, count - steps))
    return lax.ppermute(value, axis, [(source, source + steps) for source in range(first, last)])


def unit_rows(vectors):
    return vectors / jnp.sqrt(jnp.sum(vectors * vectors, axis=-1, keepdims=True) + EPS)


def unit_lower_inverse(strict_lower):
    size_all = strict_lower.shape[-1]
    positions = jnp.arange(size_all)
    inverse = jnp.broadcast_to(jnp.eye(size_all, dtype=jnp.float32), strict_lower.shape)
    size = 1
    while size < size_all:
        same_pair = positions[:, None] // (2 * size) == positions[None, :] // (2 * size)
        lower_half = ((positions[:, None] // size) % 2 == 1) & ((positions[None, :] // size) % 2 == 0)
        coupling = jnp.where(same_pair & lower_half, -strict_lower, 0.0)
        carried = jnp.einsum("hcd,hde->hce", coupling, inverse, precision=EXACT_ARITHMETIC)
        inverse = inverse + lax.optimization_barrier(
            jnp.einsum("hcd,hde->hce", inverse, carried, precision=EXACT_ARITHMETIC)
        )
        size *= 2
    return inverse


def delta_block(want_output, carry_state, block):
    query_block, key_block, value_block, beta_block, decay_block = block
    block_len = query_block.shape[1]
    cum_decay = jnp.cumsum(decay_block, axis=-1)
    positions = jnp.arange(block_len)
    lower_mask = positions[:, None] >= positions[None, :]
    strict = positions[:, None] > positions[None, :]
    decay_diff = cum_decay[:, :, None] - cum_decay[:, None, :]
    inner = jnp.where(lower_mask, jnp.exp(jnp.where(lower_mask, decay_diff, 0.0)), 0.0)
    keys_keys = jnp.einsum("hck,hdk->hcd", key_block, key_block, precision=EXACT_ARITHMETIC)
    system = jnp.eye(block_len, dtype=jnp.float32) + beta_block[:, :, None] * jnp.where(
        strict, inner * keys_keys, 0.0
    )
    growth = jnp.exp(cum_decay)
    known_part = jnp.einsum("hck,hkw->hcw", key_block, carry_state, precision=EXACT_ARITHMETIC)
    target = beta_block[:, :, None] * (value_block - growth[:, :, None] * known_part)
    update = jnp.einsum(
        "hcd,hdw->hcw", unit_lower_inverse(system - jnp.eye(block_len, dtype=jnp.float32)),
        target, precision=EXACT_ARITHMETIC,
    )
    tail_decay = jnp.exp(cum_decay[:, -1:] - cum_decay)
    new_state = growth[:, -1][:, None, None] * carry_state + jnp.einsum(
        "hck,hcw->hkw", key_block * tail_decay[:, :, None], update, precision=EXACT_ARITHMETIC
    )
    if not want_output:
        return (new_state, None)
    query_keys = jnp.einsum("hck,hdk->hcd", query_block, key_block, precision=EXACT_ARITHMETIC)
    output = growth[:, :, None] * jnp.einsum(
        "hck,hkw->hcw", query_block, carry_state, precision=EXACT_ARITHMETIC
    )
    output = output + jnp.einsum(
        "hcd,hdw->hcw", inner * query_keys, update, precision=EXACT_ARITHMETIC
    )
    return (new_state, output)


def delta_pass(queries, key_rows, values, beta_rate, decays, state_start, want_output):
    value_heads, length = beta_rate.shape
    block_count = length // STRETCH

    def to_blocks(tensor):
        shaped = tensor.reshape((value_heads, block_count, STRETCH) + tensor.shape[2:])
        return jnp.moveaxis(shaped, 1, 0)

    state_end, outputs = lax.scan(
        functools.partial(delta_block, want_output),
        state_start,
        (
            to_blocks(queries),
            to_blocks(key_rows),
            to_blocks(values),
            to_blocks(beta_rate),
            to_blocks(decays),
        ),
    )
    if want_output:
        outputs = jnp.moveaxis(outputs, 0, 1).reshape(value_heads, length, -1)
    return (state_end, outputs)


def compose(later, earlier):
    joined = jnp.einsum("...ij,...jk->...ik", later[..., :DK], earlier, precision=EXACT_ARITHMETIC)
    return joined + jnp.concatenate([jnp.zeros_like(later[..., :DK]), later[..., DK:]], axis=-1)


def within_group(value, group, offset):
    count = lax.axis_size("seq")
    pairs = [
        (start + place, start + (place + offset) % group)
        for start in range(0, count, group)
        for place in range(group)
    ]
    return lax.ppermute(value, "seq", pairs)


def entering_state(transfer, carried, init_state):
    count, position = (lax.axis_size("seq"), lax.axis_index("seq"))
    group = transfer.shape[0]
    place = position % group
    first = position == 0
    folded = (
        jnp.einsum("hij,hjk->hik", transfer, init_state, precision=EXACT_ARITHMETIC) + carried
    )
    own = jnp.concatenate(
        [
            jnp.where(first, jnp.zeros_like(transfer), transfer),
            jnp.where(first, folded, carried),
        ],
        axis=2,
    )
    items = [lax.dynamic_index_in_dim(own, place, 0, keepdims=False)]
    for offset in range(1, group):
        sent = lax.dynamic_index_in_dim(own, (place + offset) % group, 0, keepdims=False)
        items.append(within_group(sent, group, offset))
    stacked = jnp.stack(items)
    maps = jnp.take(stacked, (place - jnp.arange(group)) % group, axis=0)
    identity = jnp.concatenate(
        [jnp.eye(DK, dtype=jnp.float32), jnp.zeros((DK, DV), jnp.float32)], axis=1
    )
    prefixes = [identity]
    for member in range(group):
        prefixes.append(compose(maps[member], prefixes[-1]) if member else maps[0])
    total = prefixes.pop()
    groups = count // group
    mapping, shift = total[:, :DK], total[:, DK:]
    step = 1
    while step < groups:
        if 2 * step >= groups:
            shift_in = passed_along(shift, "seq", step * group)
            shift = jnp.dot(mapping, shift_in, precision=EXACT_ARITHMETIC) + shift
        else:
            both_in = passed_along(jnp.concatenate([mapping, shift], axis=1), "seq", step * group)
            map_in, shift_in = both_in[:, :DK], both_in[:, DK:]
            shift = jnp.dot(mapping, shift_in, precision=EXACT_ARITHMETIC) + shift
            mapping = jnp.dot(mapping, map_in, precision=EXACT_ARITHMETIC)
        step *= 2
    start_state = passed_along(shift, "seq", group) + (position < group).astype(
        jnp.float32
    ) * lax.dynamic_index_in_dim(init_state, place, 0, keepdims=False)
    prefixes = jnp.stack(prefixes)
    entering = (
        jnp.einsum("pij,jk->pik", prefixes[:, :, :DK], start_state, precision=EXACT_ARITHMETIC)
        + prefixes[:, :, DK:]
    )
    heads = [lax.dynamic_index_in_dim(entering, place, 0, keepdims=False)]
    for offset in range(1, group):
        sent = lax.dynamic_index_in_dim(entering, (place + offset) % group, 0, keepdims=False)
        heads.append(within_group(sent, group, offset))
    stacked = jnp.stack(heads)
    return jnp.take(stacked, (place - jnp.arange(group)) % group, axis=0)


def local(
    tokens_in,
    mixed_qkv,
    conv_weight,
    conv_cache,
    gate_z,
    beta_logit,
    log_decay,
    init_state,
    norm_weight,
    out_weight,
    steer_table,
    steer_index,
    post_norm_weight,
    route_ids,
    route_weight,
    w_gate_up,
    w_down,
):
    length, channels = mixed_qkv.shape
    value_heads = beta_logit.shape[0]
    group_width = 2 * DK + VALUE_HEAD_COUNT // HK * DV
    key_heads = channels // group_width
    group_size = value_heads // key_heads
    boundary_rows = passed_along(mixed_qkv[length - (KCONV - 1) :], "seq", 1)
    is_first = (lax.axis_index("seq") == 0).astype(jnp.float32)
    preceding = boundary_rows.astype(jnp.float32) + is_first * conv_cache.astype(jnp.float32)
    padded = jnp.concatenate([preceding, mixed_qkv.astype(jnp.float32)], axis=0)
    conv_taps = conv_weight.astype(jnp.float32)
    convolved = conv_taps[0] * padded[0:length]
    for offset in range(1, KCONV):
        convolved = convolved + conv_taps[offset] * padded[offset : offset + length]
    convolved = jax.nn.silu(convolved).reshape(length, key_heads, group_width)
    queries = jnp.repeat(unit_rows(convolved[:, :, :DK]) * DK ** (-0.5), group_size, axis=1)
    key_rows = jnp.repeat(unit_rows(convolved[:, :, DK : 2 * DK]), group_size, axis=1)
    values = convolved[:, :, 2 * DK :].reshape(length, value_heads, DV)
    queries = jnp.transpose(queries, (1, 0, 2))
    key_rows = jnp.transpose(key_rows, (1, 0, 2))
    values = jnp.transpose(values, (1, 0, 2))
    beta_rate = jax.nn.sigmoid(beta_logit)
    identity_maps = jnp.broadcast_to(jnp.eye(DK, dtype=jnp.float32), (value_heads, DK, DK))
    state_start = jnp.concatenate(
        [jnp.zeros((value_heads, DK, DV), jnp.float32), identity_maps], axis=2
    )
    wide_values = jnp.concatenate(
        [values, jnp.zeros((value_heads, length, DK), jnp.float32)], axis=2
    )
    state_end, wide_out = delta_pass(
        queries, key_rows, wide_values, beta_rate, log_decay, state_start, True
    )
    entering = entering_state(state_end[:, :, DV:], state_end[:, :, :DV], init_state)
    delta_out = wide_out[:, :, :DV] + jnp.einsum(
        "hlk,hkv->hlv", wide_out[:, :, DV:], entering, precision=EXACT_ARITHMETIC
    )
    delta_out = jnp.transpose(delta_out, (1, 0, 2))
    inv_rms = lax.rsqrt(jnp.mean(delta_out * delta_out, axis=-1, keepdims=True) + EPS)
    gate_act = jax.nn.silu(gate_z.astype(jnp.float32)).reshape(length, value_heads, DV)
    normed_heads = (
        (delta_out * inv_rms * norm_weight * gate_act)
        .astype(jnp.bfloat16)
        .reshape(length, value_heads * DV)
    )
    partial_value = jnp.dot(normed_heads, out_weight, preferred_element_type=jnp.float32)
    attended = lax.psum_scatter(
        partial_value.astype(jnp.bfloat16), "head", scatter_dimension=1, tiled=True
    ).astype(jnp.float32)
    hidden = tokens_in.astype(jnp.float32) + attended
    steer_onehot = (steer_index[:, None] == jnp.arange(steer_table.shape[0])[None, :]).astype(
        jnp.float32
    )
    steered = hidden + jnp.dot(
        steer_onehot, steer_table, precision=EXACT_ARITHMETIC, preferred_element_type=jnp.float32
    )
    sum_hidden, sum_steered = lax.psum(
        (jnp.sum(hidden * hidden, axis=1), jnp.sum(steered * steered, axis=1)), "head"
    )
    rescaled = steered * jnp.sqrt((sum_hidden / D + EPS) / (sum_steered / D + EPS))[:, None]
    normed = (post_norm_weight * steered * lax.rsqrt(sum_steered / D + EPS)[:, None]).astype(
        jnp.bfloat16
    )
    experts_here = w_gate_up.shape[0]
    seq_size = lax.axis_size("seq")
    experts = experts_here * seq_size
    top_count = route_ids.shape[1]
    capacity = 5 * length * top_count // (4 * experts)
    slot_count = seq_size * capacity * experts_here
    flat_ids = route_ids.reshape(-1)
    expert_hits = (flat_ids[:, None] == jnp.arange(experts, dtype=jnp.int32)[None, :]).astype(
        jnp.int32
    )
    slot_rank = jnp.sum(jnp.cumsum(expert_hits, axis=0) * expert_hits, axis=1) - 1
    owner_dev = flat_ids // experts_here
    local_expert = flat_ids % experts_here
    slot_place = (owner_dev * capacity + slot_rank) * experts_here + local_expert
    source = (
        jnp.full((slot_count,), length, jnp.int32)
        .at[slot_place]
        .set(jnp.arange(flat_ids.shape[0], dtype=jnp.int32) // top_count)
    )
    padded_rows = jnp.concatenate([normed, jnp.zeros((1, normed.shape[1]), jnp.bfloat16)], axis=0)
    outgoing = jnp.take(padded_rows, source, axis=0).reshape(seq_size, capacity, experts_here, -1)
    arrived = lax.all_to_all(outgoing, "seq", split_axis=0, concat_axis=0, tiled=True)
    row_count = seq_size * capacity
    arrived = arrived.reshape(row_count, experts_here, -1)
    ffn_width = w_down.shape[1]
    term_rows = jnp.einsum("red,edf->ref", arrived, w_gate_up, preferred_element_type=jnp.float32)
    summed = lax.psum(term_rows.reshape(row_count, -1).astype(jnp.bfloat16), "head").astype(
        jnp.float32
    )
    activate_summed = summed
    activate_summed = activate_summed.reshape(activate_summed.shape[0], experts_here, 2 * ffn_width)
    results = jnp.einsum(
        "ref,efd->red",
        (jax.nn.silu(activate_summed[:, :, :ffn_width]) * activate_summed[:, :, ffn_width:]).astype(
            jnp.bfloat16
        ),
        w_down,
        preferred_element_type=jnp.float32,
    ).astype(jnp.bfloat16)
    returned = lax.all_to_all(
        results.reshape(seq_size, capacity, experts_here, -1),
        "seq",
        split_axis=0,
        concat_axis=0,
        tiled=True,
    )
    returned = returned.reshape(slot_count, -1)
    route_mix = route_weight / jnp.sum(route_weight, axis=1, keepdims=True)
    picked = jnp.take(returned, slot_place, axis=0).reshape(length, top_count, -1)
    expert_mix = jnp.sum(picked.astype(jnp.float32) * route_mix[:, :, None], axis=1)
    return (rescaled + expert_mix).astype(jnp.bfloat16)


def solution(mesh):
    placed = (
        P("seq", "head"),
        P("seq", "head"),
        P(None, "head"),
        P(None, "head"),
        P("seq", "head"),
        P("head", "seq"),
        P("head", "seq"),
        P("head", None, None),
        P(),
        P("head", None),
        P(None, "head"),
        P("seq"),
        P("head"),
        P("seq", None),
        P("seq", None),
        P("seq", "head", None),
        P("seq", None, "head"),
    )
    return jax.shard_map(
        local, mesh=mesh, in_specs=placed, out_specs=P("seq", "head"), check_vma=False
    )
```

```python
import functools

import jax
import jax.numpy as jnp
from jax import lax
from jax.sharding import PartitionSpec as P

D = 2048
HK = 16
VALUE_HEAD_COUNT = 32
DK = 128
DV = 128
KCONV = 4
STRETCH = 128
LINK = jnp.bfloat16


EPS = 1e-06
EXACT_ARITHMETIC = lax.Precision.HIGHEST


def passed_along(value, axis, steps):
    count = lax.axis_size(axis)
    first, last = (max(0, -steps), min(count, count - steps))
    return lax.ppermute(value, axis, [(source, source + steps) for source in range(first, last)])


def unit_rows(vectors):
    return vectors / jnp.sqrt(jnp.sum(vectors * vectors, axis=-1, keepdims=True) + EPS)


def unit_lower_inverse(strict_lower):
    size_all = strict_lower.shape[-1]
    positions = jnp.arange(size_all)
    inverse = jnp.broadcast_to(jnp.eye(size_all, dtype=jnp.float32), strict_lower.shape)
    size = 1
    while size < size_all:
        same_pair = positions[:, None] // (2 * size) == positions[None, :] // (2 * size)
        lower_half = ((positions[:, None] // size) % 2 == 1) & ((positions[None, :] // size) % 2 == 0)
        coupling = jnp.where(same_pair & lower_half, -strict_lower, 0.0)
        carried = jnp.einsum("hcd,hde->hce", coupling, inverse, precision=EXACT_ARITHMETIC)
        inverse = inverse + lax.optimization_barrier(
            jnp.einsum("hcd,hde->hce", inverse, carried, precision=EXACT_ARITHMETIC)
        )
        size *= 2
    return inverse


def delta_block(want_output, carry_state, block):
    query_block, key_block, value_block, beta_block, decay_block = block
    block_len = query_block.shape[1]
    cum_decay = jnp.cumsum(decay_block, axis=-1)
    positions = jnp.arange(block_len)
    lower_mask = positions[:, None] >= positions[None, :]
    strict = positions[:, None] > positions[None, :]
    decay_diff = cum_decay[:, :, None] - cum_decay[:, None, :]
    inner = jnp.where(lower_mask, jnp.exp(jnp.where(lower_mask, decay_diff, 0.0)), 0.0)
    keys_keys = jnp.einsum("hck,hdk->hcd", key_block, key_block, precision=EXACT_ARITHMETIC)
    system = jnp.eye(block_len, dtype=jnp.float32) + beta_block[:, :, None] * jnp.where(
        strict, inner * keys_keys, 0.0
    )
    growth = jnp.exp(cum_decay)
    known_part = jnp.einsum("hck,hkw->hcw", key_block, carry_state, precision=EXACT_ARITHMETIC)
    target = beta_block[:, :, None] * (value_block - growth[:, :, None] * known_part)
    update = jnp.einsum(
        "hcd,hdw->hcw", unit_lower_inverse(system - jnp.eye(block_len, dtype=jnp.float32)),
        target, precision=EXACT_ARITHMETIC,
    )
    tail_decay = jnp.exp(cum_decay[:, -1:] - cum_decay)
    new_state = growth[:, -1][:, None, None] * carry_state + jnp.einsum(
        "hck,hcw->hkw", key_block * tail_decay[:, :, None], update, precision=EXACT_ARITHMETIC
    )
    if not want_output:
        return (new_state, None)
    query_keys = jnp.einsum("hck,hdk->hcd", query_block, key_block, precision=EXACT_ARITHMETIC)
    output = growth[:, :, None] * jnp.einsum(
        "hck,hkw->hcw", query_block, carry_state, precision=EXACT_ARITHMETIC
    )
    output = output + jnp.einsum(
        "hcd,hdw->hcw", inner * query_keys, update, precision=EXACT_ARITHMETIC
    )
    return (new_state, output)


def delta_pass(queries, key_rows, values, beta_rate, decays, state_start, want_output):
    value_heads, length = beta_rate.shape
    block_count = length // STRETCH

    def to_blocks(tensor):
        shaped = tensor.reshape((value_heads, block_count, STRETCH) + tensor.shape[2:])
        return jnp.moveaxis(shaped, 1, 0)

    state_end, outputs = lax.scan(
        functools.partial(delta_block, want_output),
        state_start,
        (
            to_blocks(queries),
            to_blocks(key_rows),
            to_blocks(values),
            to_blocks(beta_rate),
            to_blocks(decays),
        ),
    )
    if want_output:
        outputs = jnp.moveaxis(outputs, 0, 1).reshape(value_heads, length, -1)
    return (state_end, outputs)


def compose(later, earlier):
    joined = jnp.einsum("...ij,...jk->...ik", later[..., :DK], earlier, precision=EXACT_ARITHMETIC)
    return joined + jnp.concatenate([jnp.zeros_like(later[..., :DK]), later[..., DK:]], axis=-1)


def within_group(value, group, offset):
    count = lax.axis_size("seq")
    pairs = [
        (start + place, start + (place + offset) % group)
        for start in range(0, count, group)
        for place in range(group)
    ]
    return lax.ppermute(value, "seq", pairs)


def entering_state(transfer, carried, init_state):
    count, position = (lax.axis_size("seq"), lax.axis_index("seq"))
    group = transfer.shape[0]
    place = position % group
    first = position == 0
    folded = (
        jnp.einsum("hij,hjk->hik", transfer, init_state, precision=EXACT_ARITHMETIC) + carried
    )
    own = jnp.concatenate(
        [
            jnp.where(first, jnp.zeros_like(transfer), transfer),
            jnp.where(first, folded, carried),
        ],
        axis=2,
    )
    items = [lax.dynamic_index_in_dim(own, place, 0, keepdims=False)]
    for offset in range(1, group):
        sent = lax.dynamic_index_in_dim(own, (place + offset) % group, 0, keepdims=False)
        items.append(within_group(sent.astype(LINK), group, offset).astype(jnp.float32))
    stacked = jnp.stack(items)
    maps = jnp.take(stacked, (place - jnp.arange(group)) % group, axis=0)
    identity = jnp.concatenate(
        [jnp.eye(DK, dtype=jnp.float32), jnp.zeros((DK, DV), jnp.float32)], axis=1
    )
    prefixes = [identity]
    for member in range(group):
        prefixes.append(compose(maps[member], prefixes[-1]) if member else maps[0])
    total = prefixes.pop()
    groups = count // group
    mapping, shift = total[:, :DK], total[:, DK:]
    step = 1
    while step < groups:
        if 2 * step >= groups:
            shift_in = passed_along(shift.astype(LINK), "seq", step * group).astype(jnp.float32)
            shift = jnp.dot(mapping, shift_in, precision=EXACT_ARITHMETIC) + shift
        else:
            both = jnp.concatenate([mapping, shift], axis=1).astype(LINK)
            both_in = passed_along(both, "seq", step * group).astype(jnp.float32)
            map_in, shift_in = both_in[:, :DK], both_in[:, DK:]
            shift = jnp.dot(mapping, shift_in, precision=EXACT_ARITHMETIC) + shift
            mapping = jnp.dot(mapping, map_in, precision=EXACT_ARITHMETIC)
        step *= 2
    start_state = passed_along(shift, "seq", group) + (position < group).astype(
        jnp.float32
    ) * lax.dynamic_index_in_dim(init_state, place, 0, keepdims=False)
    prefixes = jnp.stack(prefixes)
    entering = (
        jnp.einsum("pij,jk->pik", prefixes[:, :, :DK], start_state, precision=EXACT_ARITHMETIC)
        + prefixes[:, :, DK:]
    )
    heads = [lax.dynamic_index_in_dim(entering, place, 0, keepdims=False)]
    for offset in range(1, group):
        sent = lax.dynamic_index_in_dim(entering, (place + offset) % group, 0, keepdims=False)
        heads.append(within_group(sent, group, offset))
    stacked = jnp.stack(heads)
    return jnp.take(stacked, (place - jnp.arange(group)) % group, axis=0)


def local(
    tokens_in,
    mixed_qkv,
    conv_weight,
    conv_cache,
    gate_z,
    beta_logit,
    log_decay,
    init_state,
    norm_weight,
    out_weight,
    steer_table,
    steer_index,
    post_norm_weight,
    route_ids,
    route_weight,
    w_gate_up,
    w_down,
):
    length, channels = mixed_qkv.shape
    value_heads = beta_logit.shape[0]
    group_width = 2 * DK + VALUE_HEAD_COUNT // HK * DV
    key_heads = channels // group_width
    group_size = value_heads // key_heads
    boundary_rows = passed_along(mixed_qkv[length - (KCONV - 1) :], "seq", 1)
    is_first = (lax.axis_index("seq") == 0).astype(jnp.float32)
    preceding = boundary_rows.astype(jnp.float32) + is_first * conv_cache.astype(jnp.float32)
    padded = jnp.concatenate([preceding, mixed_qkv.astype(jnp.float32)], axis=0)
    conv_taps = conv_weight.astype(jnp.float32)
    convolved = conv_taps[0] * padded[0:length]
    for offset in range(1, KCONV):
        convolved = convolved + conv_taps[offset] * padded[offset : offset + length]
    convolved = jax.nn.silu(convolved).reshape(length, key_heads, group_width)
    queries = jnp.repeat(unit_rows(convolved[:, :, :DK]) * DK ** (-0.5), group_size, axis=1)
    key_rows = jnp.repeat(unit_rows(convolved[:, :, DK : 2 * DK]), group_size, axis=1)
    values = convolved[:, :, 2 * DK :].reshape(length, value_heads, DV)
    queries = jnp.transpose(queries, (1, 0, 2))
    key_rows = jnp.transpose(key_rows, (1, 0, 2))
    values = jnp.transpose(values, (1, 0, 2))
    beta_rate = jax.nn.sigmoid(beta_logit)
    identity_maps = jnp.broadcast_to(jnp.eye(DK, dtype=jnp.float32), (value_heads, DK, DK))
    state_start = jnp.concatenate(
        [jnp.zeros((value_heads, DK, DV), jnp.float32), identity_maps], axis=2
    )
    wide_values = jnp.concatenate(
        [values, jnp.zeros((value_heads, length, DK), jnp.float32)], axis=2
    )
    state_end, wide_out = delta_pass(
        queries, key_rows, wide_values, beta_rate, log_decay, state_start, True
    )
    entering = entering_state(state_end[:, :, DV:], state_end[:, :, :DV], init_state)
    delta_out = wide_out[:, :, :DV] + jnp.einsum(
        "hlk,hkv->hlv", wide_out[:, :, DV:], entering, precision=EXACT_ARITHMETIC
    )
    delta_out = jnp.transpose(delta_out, (1, 0, 2))
    inv_rms = lax.rsqrt(jnp.mean(delta_out * delta_out, axis=-1, keepdims=True) + EPS)
    gate_act = jax.nn.silu(gate_z.astype(jnp.float32)).reshape(length, value_heads, DV)
    normed_heads = (
        (delta_out * inv_rms * norm_weight * gate_act)
        .astype(jnp.bfloat16)
        .reshape(length, value_heads * DV)
    )
    partial_value = jnp.dot(normed_heads, out_weight, preferred_element_type=jnp.float32)
    attended = lax.psum_scatter(
        partial_value.astype(jnp.bfloat16), "head", scatter_dimension=1, tiled=True
    ).astype(jnp.float32)
    hidden = tokens_in.astype(jnp.float32) + attended
    steer_onehot = (steer_index[:, None] == jnp.arange(steer_table.shape[0])[None, :]).astype(
        jnp.float32
    )
    steered = hidden + jnp.dot(
        steer_onehot, steer_table, precision=EXACT_ARITHMETIC, preferred_element_type=jnp.float32
    )
    sum_hidden, sum_steered = lax.psum(
        (jnp.sum(hidden * hidden, axis=1), jnp.sum(steered * steered, axis=1)), "head"
    )
    rescaled = steered * jnp.sqrt((sum_hidden / D + EPS) / (sum_steered / D + EPS))[:, None]
    normed = (post_norm_weight * steered * lax.rsqrt(sum_steered / D + EPS)[:, None]).astype(
        jnp.bfloat16
    )
    experts_here = w_gate_up.shape[0]
    seq_size = lax.axis_size("seq")
    experts = experts_here * seq_size
    top_count = route_ids.shape[1]
    capacity = 5 * length * top_count // (4 * experts)
    slot_count = seq_size * capacity * experts_here
    flat_ids = route_ids.reshape(-1)
    expert_hits = (flat_ids[:, None] == jnp.arange(experts, dtype=jnp.int32)[None, :]).astype(
        jnp.int32
    )
    slot_rank = jnp.sum(jnp.cumsum(expert_hits, axis=0) * expert_hits, axis=1) - 1
    owner_dev = flat_ids // experts_here
    local_expert = flat_ids % experts_here
    slot_place = (owner_dev * capacity + slot_rank) * experts_here + local_expert
    source = (
        jnp.full((slot_count,), length, jnp.int32)
        .at[slot_place]
        .set(jnp.arange(flat_ids.shape[0], dtype=jnp.int32) // top_count)
    )
    padded_rows = jnp.concatenate([normed, jnp.zeros((1, normed.shape[1]), jnp.bfloat16)], axis=0)
    outgoing = jnp.take(padded_rows, source, axis=0).reshape(seq_size, capacity, experts_here, -1)
    arrived = lax.all_to_all(outgoing, "seq", split_axis=0, concat_axis=0, tiled=True)
    row_count = seq_size * capacity
    arrived = arrived.reshape(row_count, experts_here, -1)
    ffn_width = w_down.shape[1]
    term_rows = jnp.einsum("red,edf->ref", arrived, w_gate_up, preferred_element_type=jnp.float32)
    summed = lax.psum(term_rows.reshape(row_count, -1).astype(jnp.bfloat16), "head").astype(
        jnp.float32
    )
    activate_summed = summed
    activate_summed = activate_summed.reshape(activate_summed.shape[0], experts_here, 2 * ffn_width)
    results = jnp.einsum(
        "ref,efd->red",
        (jax.nn.silu(activate_summed[:, :, :ffn_width]) * activate_summed[:, :, ffn_width:]).astype(
            jnp.bfloat16
        ),
        w_down,
        preferred_element_type=jnp.float32,
    ).astype(jnp.bfloat16)
    returned = lax.all_to_all(
        results.reshape(seq_size, capacity, experts_here, -1),
        "seq",
        split_axis=0,
        concat_axis=0,
        tiled=True,
    )
    returned = returned.reshape(slot_count, -1)
    route_mix = route_weight / jnp.sum(route_weight, axis=1, keepdims=True)
    picked = jnp.take(returned, slot_place, axis=0).reshape(length, top_count, -1)
    expert_mix = jnp.sum(picked.astype(jnp.float32) * route_mix[:, :, None], axis=1)
    return (rescaled + expert_mix).astype(jnp.bfloat16)


def solution(mesh):
    placed = (
        P("seq", "head"),
        P("seq", "head"),
        P(None, "head"),
        P(None, "head"),
        P("seq", "head"),
        P("head", "seq"),
        P("head", "seq"),
        P("head", None, None),
        P(),
        P("head", None),
        P(None, "head"),
        P("seq"),
        P("head"),
        P("seq", None),
        P("seq", None),
        P("seq", "head", None),
        P("seq", None, "head"),
    )
    return jax.shard_map(
        local, mesh=mesh, in_specs=placed, out_specs=P("seq", "head"), check_vma=False
    )
```

```python
import functools

import jax
import jax.numpy as jnp
from jax import lax
from jax.sharding import PartitionSpec as P

D = 2048
HK = 16
VALUE_HEAD_COUNT = 32
DK = 128
DV = 128
KCONV = 4
STRETCH = 128


EPS = 1e-06
EXACT_ARITHMETIC = lax.Precision.HIGHEST


def passed_along(value, axis, steps):
    count = lax.axis_size(axis)
    first, last = (max(0, -steps), min(count, count - steps))
    return lax.ppermute(value, axis, [(source, source + steps) for source in range(first, last)])


def unit_rows(vectors):
    return vectors / jnp.sqrt(jnp.sum(vectors * vectors, axis=-1, keepdims=True) + EPS)


def unit_lower_inverse(strict_lower):
    size_all = strict_lower.shape[-1]
    positions = jnp.arange(size_all)
    inverse = jnp.broadcast_to(jnp.eye(size_all, dtype=jnp.float32), strict_lower.shape)
    size = 1
    while size < size_all:
        same_pair = positions[:, None] // (2 * size) == positions[None, :] // (2 * size)
        lower_half = ((positions[:, None] // size) % 2 == 1) & ((positions[None, :] // size) % 2 == 0)
        coupling = jnp.where(same_pair & lower_half, -strict_lower, 0.0)
        carried = jnp.einsum("hcd,hde->hce", coupling, inverse, precision=EXACT_ARITHMETIC)
        inverse = inverse + lax.optimization_barrier(
            jnp.einsum("hcd,hde->hce", inverse, carried, precision=EXACT_ARITHMETIC)
        )
        size *= 2
    return inverse


def delta_block(want_output, carry_state, block):
    query_block, key_block, value_block, beta_block, decay_block = block
    block_len = query_block.shape[1]
    cum_decay = jnp.cumsum(decay_block, axis=-1)
    positions = jnp.arange(block_len)
    lower_mask = positions[:, None] >= positions[None, :]
    strict = positions[:, None] > positions[None, :]
    decay_diff = cum_decay[:, :, None] - cum_decay[:, None, :]
    inner = jnp.where(lower_mask, jnp.exp(jnp.where(lower_mask, decay_diff, 0.0)), 0.0)
    keys_keys = jnp.einsum("hck,hdk->hcd", key_block, key_block, precision=EXACT_ARITHMETIC)
    system = jnp.eye(block_len, dtype=jnp.float32) + beta_block[:, :, None] * jnp.where(
        strict, inner * keys_keys, 0.0
    )
    growth = jnp.exp(cum_decay)
    known_part = jnp.einsum("hck,hkw->hcw", key_block, carry_state, precision=EXACT_ARITHMETIC)
    target = beta_block[:, :, None] * (value_block - growth[:, :, None] * known_part)
    update = jnp.einsum(
        "hcd,hdw->hcw", unit_lower_inverse(system - jnp.eye(block_len, dtype=jnp.float32)),
        target, precision=EXACT_ARITHMETIC,
    )
    tail_decay = jnp.exp(cum_decay[:, -1:] - cum_decay)
    new_state = growth[:, -1][:, None, None] * carry_state + jnp.einsum(
        "hck,hcw->hkw", key_block * tail_decay[:, :, None], update, precision=EXACT_ARITHMETIC
    )
    if not want_output:
        return (new_state, None)
    query_keys = jnp.einsum("hck,hdk->hcd", query_block, key_block, precision=EXACT_ARITHMETIC)
    output = growth[:, :, None] * jnp.einsum(
        "hck,hkw->hcw", query_block, carry_state, precision=EXACT_ARITHMETIC
    )
    output = output + jnp.einsum(
        "hcd,hdw->hcw", inner * query_keys, update, precision=EXACT_ARITHMETIC
    )
    return (new_state, output)


def delta_pass(queries, key_rows, values, beta_rate, decays, state_start, want_output):
    value_heads, length = beta_rate.shape
    block_count = length // STRETCH

    def to_blocks(tensor):
        shaped = tensor.reshape((value_heads, block_count, STRETCH) + tensor.shape[2:])
        return jnp.moveaxis(shaped, 1, 0)

    state_end, outputs = lax.scan(
        functools.partial(delta_block, want_output),
        state_start,
        (
            to_blocks(queries),
            to_blocks(key_rows),
            to_blocks(values),
            to_blocks(beta_rate),
            to_blocks(decays),
        ),
    )
    if want_output:
        outputs = jnp.moveaxis(outputs, 0, 1).reshape(value_heads, length, -1)
    return (state_end, outputs)


def compose(later, earlier):
    joined = jnp.einsum("...ij,...jk->...ik", later[..., :DK], earlier, precision=EXACT_ARITHMETIC)
    return joined + jnp.concatenate([jnp.zeros_like(later[..., :DK]), later[..., DK:]], axis=-1)


def within_group(value, group, offset):
    count = lax.axis_size("seq")
    pairs = [
        (start + place, start + (place + offset) % group)
        for start in range(0, count, group)
        for place in range(group)
    ]
    return lax.ppermute(value, "seq", pairs)


def entering_state(transfer, carried, init_state):
    count, position = (lax.axis_size("seq"), lax.axis_index("seq"))
    group = transfer.shape[0]
    place = position % group
    first = position == 0
    folded = (
        jnp.einsum("hij,hjk->hik", transfer, init_state, precision=EXACT_ARITHMETIC) + carried
    )
    own = jnp.concatenate(
        [
            jnp.where(first, jnp.zeros_like(transfer), transfer),
            jnp.where(first, folded, carried),
        ],
        axis=2,
    )
    items = [lax.dynamic_index_in_dim(own, place, 0, keepdims=False)]
    for offset in range(1, group):
        sent = lax.dynamic_index_in_dim(own, (place + offset) % group, 0, keepdims=False)
        items.append(within_group(sent, group, offset))
    stacked = jnp.stack(items)
    maps = jnp.take(stacked, (place - jnp.arange(group)) % group, axis=0)
    identity = jnp.concatenate(
        [jnp.eye(DK, dtype=jnp.float32), jnp.zeros((DK, DV), jnp.float32)], axis=1
    )
    prefixes = [identity]
    for member in range(group):
        prefixes.append(compose(maps[member], prefixes[-1]) if member else maps[0])
    total = prefixes.pop()
    groups = count // group
    mapping, shift = total[:, :DK], total[:, DK:]
    step = 1
    while step < groups:
        if 2 * step >= groups:
            shift_in = passed_along(shift, "seq", step * group)
            shift = jnp.dot(mapping, shift_in, precision=EXACT_ARITHMETIC) + shift
        else:
            both_in = passed_along(jnp.concatenate([mapping, shift], axis=1), "seq", step * group)
            map_in, shift_in = both_in[:, :DK], both_in[:, DK:]
            shift = jnp.dot(mapping, shift_in, precision=EXACT_ARITHMETIC) + shift
            mapping = jnp.dot(mapping, map_in, precision=EXACT_ARITHMETIC)
        step *= 2
    start_state = passed_along(shift, "seq", group) + (position < group).astype(
        jnp.float32
    ) * lax.dynamic_index_in_dim(init_state, place, 0, keepdims=False)
    prefixes = jnp.stack(prefixes)
    entering = (
        jnp.einsum("pij,jk->pik", prefixes[:, :, :DK], start_state, precision=EXACT_ARITHMETIC)
        + prefixes[:, :, DK:]
    )
    heads = [lax.dynamic_index_in_dim(entering, place, 0, keepdims=False)]
    for offset in range(1, group):
        sent = lax.dynamic_index_in_dim(entering, (place + offset) % group, 0, keepdims=False)
        heads.append(within_group(sent, group, offset))
    stacked = jnp.stack(heads)
    return jnp.take(stacked, (place - jnp.arange(group)) % group, axis=0)


def local(
    tokens_in,
    mixed_qkv,
    conv_weight,
    conv_cache,
    gate_z,
    beta_logit,
    log_decay,
    init_state,
    norm_weight,
    out_weight,
    steer_table,
    steer_index,
    post_norm_weight,
    route_ids,
    route_weight,
    w_gate_up,
    w_down,
):
    length, channels = mixed_qkv.shape
    value_heads = beta_logit.shape[0]
    group_width = 2 * DK + VALUE_HEAD_COUNT // HK * DV
    key_heads = channels // group_width
    group_size = value_heads // key_heads
    boundary_rows = passed_along(mixed_qkv[length - (KCONV - 1) :], "seq", 1)
    is_first = (lax.axis_index("seq") == 0).astype(jnp.float32)
    preceding = boundary_rows.astype(jnp.float32) + is_first * conv_cache.astype(jnp.float32)
    padded = jnp.concatenate([preceding, mixed_qkv.astype(jnp.float32)], axis=0)
    conv_taps = conv_weight.astype(jnp.float32)
    convolved = conv_taps[0] * padded[0:length]
    for offset in range(1, KCONV):
        convolved = convolved + conv_taps[offset] * padded[offset : offset + length]
    convolved = jax.nn.silu(convolved).reshape(length, key_heads, group_width)
    queries = jnp.repeat(unit_rows(convolved[:, :, :DK]) * DK ** (-0.5), group_size, axis=1)
    key_rows = jnp.repeat(unit_rows(convolved[:, :, DK : 2 * DK]), group_size, axis=1)
    values = convolved[:, :, 2 * DK :].reshape(length, value_heads, DV)
    queries = jnp.transpose(queries, (1, 0, 2))
    key_rows = jnp.transpose(key_rows, (1, 0, 2))
    values = jnp.transpose(values, (1, 0, 2))
    beta_rate = jax.nn.sigmoid(beta_logit)
    identity_maps = jnp.broadcast_to(jnp.eye(DK, dtype=jnp.float32), (value_heads, DK, DK))
    state_start = jnp.concatenate(
        [jnp.zeros((value_heads, DK, DV), jnp.float32), identity_maps], axis=2
    )
    wide_values = jnp.concatenate(
        [values, jnp.zeros((value_heads, length, DK), jnp.float32)], axis=2
    )
    state_end, wide_out = delta_pass(
        queries, key_rows, wide_values, beta_rate, log_decay, state_start, True
    )
    entering = entering_state(state_end[:, :, DV:], state_end[:, :, :DV], init_state)
    delta_out = wide_out[:, :, :DV] + jnp.einsum(
        "hlk,hkv->hlv", wide_out[:, :, DV:], entering, precision=EXACT_ARITHMETIC
    )
    delta_out = jnp.transpose(delta_out, (1, 0, 2))
    inv_rms = lax.rsqrt(jnp.mean(delta_out * delta_out, axis=-1, keepdims=True) + EPS)
    gate_act = jax.nn.silu(gate_z.astype(jnp.float32)).reshape(length, value_heads, DV)
    normed_heads = (
        (delta_out * inv_rms * norm_weight * gate_act)
        .astype(jnp.bfloat16)
        .reshape(length, value_heads * DV)
    )
    partial_value = jnp.dot(normed_heads, out_weight, preferred_element_type=jnp.float32)
    head_count = lax.axis_size("head")
    blocks = partial_value.astype(jnp.bfloat16).reshape(length, head_count, -1)
    blocks = lax.all_to_all(
        jnp.transpose(blocks, (1, 0, 2)), "head", split_axis=0, concat_axis=0, tiled=True
    )
    attended = jnp.sum(blocks.astype(jnp.float32), axis=0)
    hidden = tokens_in.astype(jnp.float32) + attended
    steer_onehot = (steer_index[:, None] == jnp.arange(steer_table.shape[0])[None, :]).astype(
        jnp.float32
    )
    steered = hidden + jnp.dot(
        steer_onehot, steer_table, precision=EXACT_ARITHMETIC, preferred_element_type=jnp.float32
    )
    sum_hidden, sum_steered = lax.psum(
        (jnp.sum(hidden * hidden, axis=1), jnp.sum(steered * steered, axis=1)), "head"
    )
    rescaled = steered * jnp.sqrt((sum_hidden / D + EPS) / (sum_steered / D + EPS))[:, None]
    normed = (post_norm_weight * steered * lax.rsqrt(sum_steered / D + EPS)[:, None]).astype(
        jnp.bfloat16
    )
    experts_here = w_gate_up.shape[0]
    seq_size = lax.axis_size("seq")
    experts = experts_here * seq_size
    top_count = route_ids.shape[1]
    capacity = 5 * length * top_count // (4 * experts)
    slot_count = seq_size * capacity * experts_here
    flat_ids = route_ids.reshape(-1)
    expert_hits = (flat_ids[:, None] == jnp.arange(experts, dtype=jnp.int32)[None, :]).astype(
        jnp.int32
    )
    slot_rank = jnp.sum(jnp.cumsum(expert_hits, axis=0) * expert_hits, axis=1) - 1
    owner_dev = flat_ids // experts_here
    local_expert = flat_ids % experts_here
    slot_place = (owner_dev * capacity + slot_rank) * experts_here + local_expert
    source = (
        jnp.full((slot_count,), length, jnp.int32)
        .at[slot_place]
        .set(jnp.arange(flat_ids.shape[0], dtype=jnp.int32) // top_count)
    )
    padded_rows = jnp.concatenate([normed, jnp.zeros((1, normed.shape[1]), jnp.bfloat16)], axis=0)
    outgoing = jnp.take(padded_rows, source, axis=0).reshape(seq_size, capacity, experts_here, -1)
    arrived = lax.all_to_all(outgoing, "seq", split_axis=0, concat_axis=0, tiled=True)
    row_count = seq_size * capacity
    arrived = arrived.reshape(row_count, experts_here, -1)
    ffn_width = w_down.shape[1]
    term_rows = jnp.einsum("red,edf->ref", arrived, w_gate_up, preferred_element_type=jnp.float32)
    summed = lax.psum(term_rows.reshape(row_count, -1).astype(jnp.bfloat16), "head").astype(
        jnp.float32
    )
    activate_summed = summed
    activate_summed = activate_summed.reshape(activate_summed.shape[0], experts_here, 2 * ffn_width)
    results = jnp.einsum(
        "ref,efd->red",
        (jax.nn.silu(activate_summed[:, :, :ffn_width]) * activate_summed[:, :, ffn_width:]).astype(
            jnp.bfloat16
        ),
        w_down,
        preferred_element_type=jnp.float32,
    ).astype(jnp.bfloat16)
    returned = lax.all_to_all(
        results.reshape(seq_size, capacity, experts_here, -1),
        "seq",
        split_axis=0,
        concat_axis=0,
        tiled=True,
    )
    returned = returned.reshape(slot_count, -1)
    route_mix = route_weight / jnp.sum(route_weight, axis=1, keepdims=True)
    picked = jnp.take(returned, slot_place, axis=0).reshape(length, top_count, -1)
    expert_mix = jnp.sum(picked.astype(jnp.float32) * route_mix[:, :, None], axis=1)
    return (rescaled + expert_mix).astype(jnp.bfloat16)


def solution(mesh):
    placed = (
        P("seq", "head"),
        P("seq", "head"),
        P(None, "head"),
        P(None, "head"),
        P("seq", "head"),
        P("head", "seq"),
        P("head", "seq"),
        P("head", None, None),
        P(),
        P("head", None),
        P(None, "head"),
        P("seq"),
        P("head"),
        P("seq", None),
        P("seq", None),
        P("seq", "head", None),
        P("seq", None, "head"),
    )
    return jax.shard_map(
        local, mesh=mesh, in_specs=placed, out_specs=P("seq", "head"), check_vma=False
    )
```

```python
import functools

import jax
import jax.numpy as jnp
from jax import lax
from jax.sharding import PartitionSpec as P

D = 2048
HK = 16
VALUE_HEAD_COUNT = 32
DK = 128
DV = 128
KCONV = 4
STRETCH = 128


EPS = 1e-06
EXACT_ARITHMETIC = lax.Precision.HIGHEST


def passed_along(value, axis, steps):
    count = lax.axis_size(axis)
    first, last = (max(0, -steps), min(count, count - steps))
    return lax.ppermute(value, axis, [(source, source + steps) for source in range(first, last)])


def unit_rows(vectors):
    return vectors / jnp.sqrt(jnp.sum(vectors * vectors, axis=-1, keepdims=True) + EPS)


def unit_lower_inverse(strict_lower):
    size_all = strict_lower.shape[-1]
    positions = jnp.arange(size_all)
    inverse = jnp.broadcast_to(jnp.eye(size_all, dtype=jnp.float32), strict_lower.shape)
    size = 1
    while size < size_all:
        same_pair = positions[:, None] // (2 * size) == positions[None, :] // (2 * size)
        lower_half = ((positions[:, None] // size) % 2 == 1) & ((positions[None, :] // size) % 2 == 0)
        coupling = jnp.where(same_pair & lower_half, -strict_lower, 0.0)
        carried = jnp.einsum("hcd,hde->hce", coupling, inverse, precision=EXACT_ARITHMETIC)
        inverse = inverse + lax.optimization_barrier(
            jnp.einsum("hcd,hde->hce", inverse, carried, precision=EXACT_ARITHMETIC)
        )
        size *= 2
    return inverse


def delta_block(want_output, carry_state, block):
    query_block, key_block, value_block, beta_block, decay_block = block
    block_len = query_block.shape[1]
    cum_decay = jnp.cumsum(decay_block, axis=-1)
    positions = jnp.arange(block_len)
    lower_mask = positions[:, None] >= positions[None, :]
    strict = positions[:, None] > positions[None, :]
    decay_diff = cum_decay[:, :, None] - cum_decay[:, None, :]
    inner = jnp.where(lower_mask, jnp.exp(jnp.where(lower_mask, decay_diff, 0.0)), 0.0)
    keys_keys = jnp.einsum("hck,hdk->hcd", key_block, key_block, precision=EXACT_ARITHMETIC)
    system = jnp.eye(block_len, dtype=jnp.float32) + beta_block[:, :, None] * jnp.where(
        strict, inner * keys_keys, 0.0
    )
    growth = jnp.exp(cum_decay)
    known_part = jnp.einsum("hck,hkw->hcw", key_block, carry_state, precision=EXACT_ARITHMETIC)
    target = beta_block[:, :, None] * (value_block - growth[:, :, None] * known_part)
    update = jnp.einsum(
        "hcd,hdw->hcw", unit_lower_inverse(system - jnp.eye(block_len, dtype=jnp.float32)),
        target, precision=EXACT_ARITHMETIC,
    )
    tail_decay = jnp.exp(cum_decay[:, -1:] - cum_decay)
    new_state = growth[:, -1][:, None, None] * carry_state + jnp.einsum(
        "hck,hcw->hkw", key_block * tail_decay[:, :, None], update, precision=EXACT_ARITHMETIC
    )
    if not want_output:
        return (new_state, None)
    query_keys = jnp.einsum("hck,hdk->hcd", query_block, key_block, precision=EXACT_ARITHMETIC)
    output = growth[:, :, None] * jnp.einsum(
        "hck,hkw->hcw", query_block, carry_state, precision=EXACT_ARITHMETIC
    )
    output = output + jnp.einsum(
        "hcd,hdw->hcw", inner * query_keys, update, precision=EXACT_ARITHMETIC
    )
    return (new_state, output)


def delta_pass(queries, key_rows, values, beta_rate, decays, state_start, want_output):
    value_heads, length = beta_rate.shape
    block_count = length // STRETCH

    def to_blocks(tensor):
        shaped = tensor.reshape((value_heads, block_count, STRETCH) + tensor.shape[2:])
        return jnp.moveaxis(shaped, 1, 0)

    state_end, outputs = lax.scan(
        functools.partial(delta_block, want_output),
        state_start,
        (
            to_blocks(queries),
            to_blocks(key_rows),
            to_blocks(values),
            to_blocks(beta_rate),
            to_blocks(decays),
        ),
    )
    if want_output:
        outputs = jnp.moveaxis(outputs, 0, 1).reshape(value_heads, length, -1)
    return (state_end, outputs)


def compose(later, earlier):
    joined = jnp.einsum("...ij,...jk->...ik", later[..., :DK], earlier, precision=EXACT_ARITHMETIC)
    return joined + jnp.concatenate([jnp.zeros_like(later[..., :DK]), later[..., DK:]], axis=-1)


def within_group(value, group, offset):
    count = lax.axis_size("seq")
    pairs = [
        (start + place, start + (place + offset) % group)
        for start in range(0, count, group)
        for place in range(group)
    ]
    return lax.ppermute(value, "seq", pairs)


def entering_state(transfer, carried, init_state):
    count, position = (lax.axis_size("seq"), lax.axis_index("seq"))
    group = transfer.shape[0]
    place = position % group
    first = position == 0
    folded = (
        jnp.einsum("hij,hjk->hik", transfer, init_state, precision=EXACT_ARITHMETIC) + carried
    )
    own = jnp.concatenate(
        [
            jnp.where(first, jnp.zeros_like(transfer), transfer),
            jnp.where(first, folded, carried),
        ],
        axis=2,
    )
    items = [lax.dynamic_index_in_dim(own, place, 0, keepdims=False)]
    for offset in range(1, group):
        sent = lax.dynamic_index_in_dim(own, (place + offset) % group, 0, keepdims=False)
        items.append(within_group(sent, group, offset))
    stacked = jnp.stack(items)
    maps = jnp.take(stacked, (place - jnp.arange(group)) % group, axis=0)
    identity = jnp.concatenate(
        [jnp.eye(DK, dtype=jnp.float32), jnp.zeros((DK, DV), jnp.float32)], axis=1
    )
    prefixes = [identity]
    for member in range(group):
        prefixes.append(compose(maps[member], prefixes[-1]) if member else maps[0])
    total = prefixes.pop()
    groups = count // group
    mapping, shift = total[:, :DK], total[:, DK:]
    step = 1
    while step < groups:
        if 2 * step >= groups:
            shift_in = passed_along(shift, "seq", step * group)
            shift = jnp.dot(mapping, shift_in, precision=EXACT_ARITHMETIC) + shift
        else:
            both_in = passed_along(jnp.concatenate([mapping, shift], axis=1), "seq", step * group)
            map_in, shift_in = both_in[:, :DK], both_in[:, DK:]
            shift = jnp.dot(mapping, shift_in, precision=EXACT_ARITHMETIC) + shift
            mapping = jnp.dot(mapping, map_in, precision=EXACT_ARITHMETIC)
        step *= 2
    start_state = passed_along(shift, "seq", group) + (position < group).astype(
        jnp.float32
    ) * lax.dynamic_index_in_dim(init_state, place, 0, keepdims=False)
    prefixes = jnp.stack(prefixes)
    entering = (
        jnp.einsum("pij,jk->pik", prefixes[:, :, :DK], start_state, precision=EXACT_ARITHMETIC)
        + prefixes[:, :, DK:]
    )
    heads = [lax.dynamic_index_in_dim(entering, place, 0, keepdims=False)]
    for offset in range(1, group):
        sent = lax.dynamic_index_in_dim(entering, (place + offset) % group, 0, keepdims=False)
        heads.append(within_group(sent, group, offset))
    stacked = jnp.stack(heads)
    return jnp.take(stacked, (place - jnp.arange(group)) % group, axis=0)


def local(
    tokens_in,
    mixed_qkv,
    conv_weight,
    conv_cache,
    gate_z,
    beta_logit,
    log_decay,
    init_state,
    norm_weight,
    out_weight,
    steer_table,
    steer_index,
    post_norm_weight,
    route_ids,
    route_weight,
    w_gate_up,
    w_down,
):
    length, channels = mixed_qkv.shape
    value_heads = beta_logit.shape[0]
    group_width = 2 * DK + VALUE_HEAD_COUNT // HK * DV
    key_heads = channels // group_width
    group_size = value_heads // key_heads
    boundary_rows = passed_along(mixed_qkv[length - (KCONV - 1) :], "seq", 1)
    is_first = (lax.axis_index("seq") == 0).astype(jnp.float32)
    preceding = boundary_rows.astype(jnp.float32) + is_first * conv_cache.astype(jnp.float32)
    padded = jnp.concatenate([preceding, mixed_qkv.astype(jnp.float32)], axis=0)
    conv_taps = conv_weight.astype(jnp.float32)
    convolved = conv_taps[0] * padded[0:length]
    for offset in range(1, KCONV):
        convolved = convolved + conv_taps[offset] * padded[offset : offset + length]
    convolved = jax.nn.silu(convolved).reshape(length, key_heads, group_width)
    queries = jnp.repeat(unit_rows(convolved[:, :, :DK]) * DK ** (-0.5), group_size, axis=1)
    key_rows = jnp.repeat(unit_rows(convolved[:, :, DK : 2 * DK]), group_size, axis=1)
    values = convolved[:, :, 2 * DK :].reshape(length, value_heads, DV)
    queries = jnp.transpose(queries, (1, 0, 2))
    key_rows = jnp.transpose(key_rows, (1, 0, 2))
    values = jnp.transpose(values, (1, 0, 2))
    beta_rate = jax.nn.sigmoid(beta_logit)
    identity_maps = jnp.broadcast_to(jnp.eye(DK, dtype=jnp.float32), (value_heads, DK, DK))
    state_start = jnp.concatenate(
        [jnp.zeros((value_heads, DK, DV), jnp.float32), identity_maps], axis=2
    )
    wide_values = jnp.concatenate(
        [values, jnp.zeros((value_heads, length, DK), jnp.float32)], axis=2
    )
    state_end, wide_out = delta_pass(
        queries, key_rows, wide_values, beta_rate, log_decay, state_start, True
    )
    entering = entering_state(state_end[:, :, DV:], state_end[:, :, :DV], init_state)
    delta_out = wide_out[:, :, :DV] + jnp.einsum(
        "hlk,hkv->hlv", wide_out[:, :, DV:], entering, precision=EXACT_ARITHMETIC
    )
    delta_out = jnp.transpose(delta_out, (1, 0, 2))
    inv_rms = lax.rsqrt(jnp.mean(delta_out * delta_out, axis=-1, keepdims=True) + EPS)
    gate_act = jax.nn.silu(gate_z.astype(jnp.float32)).reshape(length, value_heads, DV)
    normed_heads = (
        (delta_out * inv_rms * norm_weight * gate_act)
        .astype(jnp.bfloat16)
        .reshape(length, value_heads * DV)
    )
    partial_value = jnp.dot(normed_heads, out_weight, preferred_element_type=jnp.float32)
    head_count = lax.axis_size("head")
    blocks = partial_value.astype(jnp.bfloat16).reshape(length, head_count, -1)
    blocks = lax.all_to_all(
        jnp.transpose(blocks, (1, 0, 2)), "head", split_axis=0, concat_axis=0, tiled=True
    )
    attended = jnp.sum(blocks.astype(jnp.float32), axis=0)
    hidden = tokens_in.astype(jnp.float32) + attended
    steer_onehot = (steer_index[:, None] == jnp.arange(steer_table.shape[0])[None, :]).astype(
        jnp.float32
    )
    steered = hidden + jnp.dot(
        steer_onehot, steer_table, precision=EXACT_ARITHMETIC, preferred_element_type=jnp.float32
    )
    sum_hidden, sum_steered = lax.psum(
        (jnp.sum(hidden * hidden, axis=1), jnp.sum(steered * steered, axis=1)), "head"
    )
    rescaled = steered * jnp.sqrt((sum_hidden / D + EPS) / (sum_steered / D + EPS))[:, None]
    normed = (post_norm_weight * steered * lax.rsqrt(sum_steered / D + EPS)[:, None]).astype(
        jnp.bfloat16
    )
    experts_here = w_gate_up.shape[0]
    seq_size = lax.axis_size("seq")
    experts = experts_here * seq_size
    top_count = route_ids.shape[1]
    capacity = 5 * length * top_count // (4 * experts)
    slot_count = seq_size * capacity * experts_here
    flat_ids = route_ids.reshape(-1)
    expert_hits = (flat_ids[:, None] == jnp.arange(experts, dtype=jnp.int32)[None, :]).astype(
        jnp.int32
    )
    slot_rank = jnp.sum(jnp.cumsum(expert_hits, axis=0) * expert_hits, axis=1) - 1
    owner_dev = flat_ids // experts_here
    local_expert = flat_ids % experts_here
    slot_place = (owner_dev * capacity + slot_rank) * experts_here + local_expert
    source = (
        jnp.full((slot_count,), length, jnp.int32)
        .at[slot_place]
        .set(jnp.arange(flat_ids.shape[0], dtype=jnp.int32) // top_count)
    )
    padded_rows = jnp.concatenate([normed, jnp.zeros((1, normed.shape[1]), jnp.bfloat16)], axis=0)
    outgoing = jnp.take(padded_rows, source, axis=0).reshape(seq_size, capacity, experts_here, -1)
    arrived = lax.all_to_all(outgoing, "seq", split_axis=0, concat_axis=0, tiled=True)
    row_count = seq_size * capacity
    arrived = arrived.reshape(row_count, experts_here, -1)
    ffn_width = w_down.shape[1]
    term_rows = jnp.einsum("red,edf->ref", arrived, w_gate_up, preferred_element_type=jnp.float32)
    head_count = lax.axis_size("head")
    slice_width = ffn_width // head_count
    pieces = term_rows.astype(jnp.bfloat16).reshape(
        row_count, experts_here, 2, head_count, slice_width
    )
    pieces = lax.all_to_all(
        jnp.transpose(pieces, (3, 0, 1, 2, 4)), "head", split_axis=0, concat_axis=0, tiled=True
    )
    gate_up_slice = jnp.sum(pieces.astype(jnp.float32), axis=0)
    activated_slice = (jax.nn.silu(gate_up_slice[:, :, 0]) * gate_up_slice[:, :, 1]).astype(
        jnp.bfloat16
    )
    activated = lax.all_to_all(
        jnp.broadcast_to(activated_slice[None], (head_count,) + activated_slice.shape),
        "head",
        split_axis=0,
        concat_axis=0,
        tiled=True,
    )
    activated = jnp.transpose(activated, (1, 2, 0, 3)).reshape(row_count, experts_here, ffn_width)
    results = jnp.einsum(
        "ref,efd->red", activated, w_down, preferred_element_type=jnp.float32
    ).astype(jnp.bfloat16)
    returned = lax.all_to_all(
        results.reshape(seq_size, capacity, experts_here, -1),
        "seq",
        split_axis=0,
        concat_axis=0,
        tiled=True,
    )
    returned = returned.reshape(slot_count, -1)
    route_mix = route_weight / jnp.sum(route_weight, axis=1, keepdims=True)
    picked = jnp.take(returned, slot_place, axis=0).reshape(length, top_count, -1)
    expert_mix = jnp.sum(picked.astype(jnp.float32) * route_mix[:, :, None], axis=1)
    return (rescaled + expert_mix).astype(jnp.bfloat16)


def solution(mesh):
    placed = (
        P("seq", "head"),
        P("seq", "head"),
        P(None, "head"),
        P(None, "head"),
        P("seq", "head"),
        P("head", "seq"),
        P("head", "seq"),
        P("head", None, None),
        P(),
        P("head", None),
        P(None, "head"),
        P("seq"),
        P("head"),
        P("seq", None),
        P("seq", None),
        P("seq", "head", None),
        P("seq", None, "head"),
    )
    return jax.shard_map(
        local, mesh=mesh, in_specs=placed, out_specs=P("seq", "head"), check_vma=False
    )
```

```python
import functools

import jax
import jax.numpy as jnp
from jax import lax
from jax.sharding import PartitionSpec as P

D = 2048
HK = 16
VALUE_HEAD_COUNT = 32
DK = 128
DV = 128
KCONV = 4
STRETCH = 128
SCAN_RADIX = 4


EPS = 1e-06
EXACT_ARITHMETIC = lax.Precision.HIGHEST


def passed_along(value, axis, steps):
    count = lax.axis_size(axis)
    first, last = (max(0, -steps), min(count, count - steps))
    return lax.ppermute(value, axis, [(source, source + steps) for source in range(first, last)])


def unit_rows(vectors):
    return vectors / jnp.sqrt(jnp.sum(vectors * vectors, axis=-1, keepdims=True) + EPS)


def unit_lower_inverse(strict_lower):
    size_all = strict_lower.shape[-1]
    positions = jnp.arange(size_all)
    inverse = jnp.broadcast_to(jnp.eye(size_all, dtype=jnp.float32), strict_lower.shape)
    size = 1
    while size < size_all:
        same_pair = positions[:, None] // (2 * size) == positions[None, :] // (2 * size)
        lower_half = ((positions[:, None] // size) % 2 == 1) & ((positions[None, :] // size) % 2 == 0)
        coupling = jnp.where(same_pair & lower_half, -strict_lower, 0.0)
        carried = jnp.einsum("hcd,hde->hce", coupling, inverse, precision=EXACT_ARITHMETIC)
        inverse = inverse + lax.optimization_barrier(
            jnp.einsum("hcd,hde->hce", inverse, carried, precision=EXACT_ARITHMETIC)
        )
        size *= 2
    return inverse


def delta_block(want_output, carry_state, block):
    query_block, key_block, value_block, beta_block, decay_block = block
    block_len = query_block.shape[1]
    cum_decay = jnp.cumsum(decay_block, axis=-1)
    positions = jnp.arange(block_len)
    lower_mask = positions[:, None] >= positions[None, :]
    strict = positions[:, None] > positions[None, :]
    decay_diff = cum_decay[:, :, None] - cum_decay[:, None, :]
    inner = jnp.where(lower_mask, jnp.exp(jnp.where(lower_mask, decay_diff, 0.0)), 0.0)
    keys_keys = jnp.einsum("hck,hdk->hcd", key_block, key_block, precision=EXACT_ARITHMETIC)
    system = jnp.eye(block_len, dtype=jnp.float32) + beta_block[:, :, None] * jnp.where(
        strict, inner * keys_keys, 0.0
    )
    growth = jnp.exp(cum_decay)
    known_part = jnp.einsum("hck,hkw->hcw", key_block, carry_state, precision=EXACT_ARITHMETIC)
    target = beta_block[:, :, None] * (value_block - growth[:, :, None] * known_part)
    update = jnp.einsum(
        "hcd,hdw->hcw", unit_lower_inverse(system - jnp.eye(block_len, dtype=jnp.float32)),
        target, precision=EXACT_ARITHMETIC,
    )
    tail_decay = jnp.exp(cum_decay[:, -1:] - cum_decay)
    new_state = growth[:, -1][:, None, None] * carry_state + jnp.einsum(
        "hck,hcw->hkw", key_block * tail_decay[:, :, None], update, precision=EXACT_ARITHMETIC
    )
    if not want_output:
        return (new_state, None)
    query_keys = jnp.einsum("hck,hdk->hcd", query_block, key_block, precision=EXACT_ARITHMETIC)
    output = growth[:, :, None] * jnp.einsum(
        "hck,hkw->hcw", query_block, carry_state, precision=EXACT_ARITHMETIC
    )
    output = output + jnp.einsum(
        "hcd,hdw->hcw", inner * query_keys, update, precision=EXACT_ARITHMETIC
    )
    return (new_state, output)


def delta_pass(queries, key_rows, values, beta_rate, decays, state_start, want_output):
    value_heads, length = beta_rate.shape
    block_count = length // STRETCH

    def to_blocks(tensor):
        shaped = tensor.reshape((value_heads, block_count, STRETCH) + tensor.shape[2:])
        return jnp.moveaxis(shaped, 1, 0)

    state_end, outputs = lax.scan(
        functools.partial(delta_block, want_output),
        state_start,
        (
            to_blocks(queries),
            to_blocks(key_rows),
            to_blocks(values),
            to_blocks(beta_rate),
            to_blocks(decays),
        ),
    )
    if want_output:
        outputs = jnp.moveaxis(outputs, 0, 1).reshape(value_heads, length, -1)
    return (state_end, outputs)


def compose(later, earlier):
    joined = jnp.einsum("...ij,...jk->...ik", later[..., :DK], earlier, precision=EXACT_ARITHMETIC)
    return joined + jnp.concatenate([jnp.zeros_like(later[..., :DK]), later[..., DK:]], axis=-1)


def within_group(value, group, offset):
    count = lax.axis_size("seq")
    pairs = [
        (start + place, start + (place + offset) % group)
        for start in range(0, count, group)
        for place in range(group)
    ]
    return lax.ppermute(value, "seq", pairs)


def entering_state(transfer, carried, init_state):
    count, position = (lax.axis_size("seq"), lax.axis_index("seq"))
    group = transfer.shape[0]
    place = position % group
    first = position == 0
    folded = (
        jnp.einsum("hij,hjk->hik", transfer, init_state, precision=EXACT_ARITHMETIC) + carried
    )
    own = jnp.concatenate(
        [
            jnp.where(first, jnp.zeros_like(transfer), transfer),
            jnp.where(first, folded, carried),
        ],
        axis=2,
    )
    items = [lax.dynamic_index_in_dim(own, place, 0, keepdims=False)]
    for offset in range(1, group):
        sent = lax.dynamic_index_in_dim(own, (place + offset) % group, 0, keepdims=False)
        items.append(within_group(sent, group, offset))
    stacked = jnp.stack(items)
    maps = jnp.take(stacked, (place - jnp.arange(group)) % group, axis=0)
    identity = jnp.concatenate(
        [jnp.eye(DK, dtype=jnp.float32), jnp.zeros((DK, DV), jnp.float32)], axis=1
    )
    prefixes = [identity]
    for member in range(group):
        prefixes.append(compose(maps[member], prefixes[-1]) if member else maps[0])
    total = prefixes.pop()
    groups = count // group
    inclusive = total
    exclusive = None
    span = 1
    while span < groups:
        for hop in range(1, SCAN_RADIX):
            if span * hop < groups:
                part = passed_along(inclusive, "seq", span * hop * group)
                exclusive = part if exclusive is None else compose(exclusive, part)
        span *= SCAN_RADIX
        if span < groups:
            inclusive = compose(total, exclusive)
    start_state = jnp.where(
        position < group,
        lax.dynamic_index_in_dim(init_state, place, 0, keepdims=False),
        exclusive[:, DK:],
    )
    prefixes = jnp.stack(prefixes)
    entering = (
        jnp.einsum("pij,jk->pik", prefixes[:, :, :DK], start_state, precision=EXACT_ARITHMETIC)
        + prefixes[:, :, DK:]
    )
    heads = [lax.dynamic_index_in_dim(entering, place, 0, keepdims=False)]
    for offset in range(1, group):
        sent = lax.dynamic_index_in_dim(entering, (place + offset) % group, 0, keepdims=False)
        heads.append(within_group(sent, group, offset))
    stacked = jnp.stack(heads)
    return jnp.take(stacked, (place - jnp.arange(group)) % group, axis=0)


def local(
    tokens_in,
    mixed_qkv,
    conv_weight,
    conv_cache,
    gate_z,
    beta_logit,
    log_decay,
    init_state,
    norm_weight,
    out_weight,
    steer_table,
    steer_index,
    post_norm_weight,
    route_ids,
    route_weight,
    w_gate_up,
    w_down,
):
    length, channels = mixed_qkv.shape
    value_heads = beta_logit.shape[0]
    group_width = 2 * DK + VALUE_HEAD_COUNT // HK * DV
    key_heads = channels // group_width
    group_size = value_heads // key_heads
    boundary_rows = passed_along(mixed_qkv[length - (KCONV - 1) :], "seq", 1)
    is_first = (lax.axis_index("seq") == 0).astype(jnp.float32)
    preceding = boundary_rows.astype(jnp.float32) + is_first * conv_cache.astype(jnp.float32)
    padded = jnp.concatenate([preceding, mixed_qkv.astype(jnp.float32)], axis=0)
    conv_taps = conv_weight.astype(jnp.float32)
    convolved = conv_taps[0] * padded[0:length]
    for offset in range(1, KCONV):
        convolved = convolved + conv_taps[offset] * padded[offset : offset + length]
    convolved = jax.nn.silu(convolved).reshape(length, key_heads, group_width)
    queries = jnp.repeat(unit_rows(convolved[:, :, :DK]) * DK ** (-0.5), group_size, axis=1)
    key_rows = jnp.repeat(unit_rows(convolved[:, :, DK : 2 * DK]), group_size, axis=1)
    values = convolved[:, :, 2 * DK :].reshape(length, value_heads, DV)
    queries = jnp.transpose(queries, (1, 0, 2))
    key_rows = jnp.transpose(key_rows, (1, 0, 2))
    values = jnp.transpose(values, (1, 0, 2))
    beta_rate = jax.nn.sigmoid(beta_logit)
    identity_maps = jnp.broadcast_to(jnp.eye(DK, dtype=jnp.float32), (value_heads, DK, DK))
    state_start = jnp.concatenate(
        [jnp.zeros((value_heads, DK, DV), jnp.float32), identity_maps], axis=2
    )
    wide_values = jnp.concatenate(
        [values, jnp.zeros((value_heads, length, DK), jnp.float32)], axis=2
    )
    state_end, wide_out = delta_pass(
        queries, key_rows, wide_values, beta_rate, log_decay, state_start, True
    )
    entering = entering_state(state_end[:, :, DV:], state_end[:, :, :DV], init_state)
    delta_out = wide_out[:, :, :DV] + jnp.einsum(
        "hlk,hkv->hlv", wide_out[:, :, DV:], entering, precision=EXACT_ARITHMETIC
    )
    delta_out = jnp.transpose(delta_out, (1, 0, 2))
    inv_rms = lax.rsqrt(jnp.mean(delta_out * delta_out, axis=-1, keepdims=True) + EPS)
    gate_act = jax.nn.silu(gate_z.astype(jnp.float32)).reshape(length, value_heads, DV)
    normed_heads = (
        (delta_out * inv_rms * norm_weight * gate_act)
        .astype(jnp.bfloat16)
        .reshape(length, value_heads * DV)
    )
    partial_value = jnp.dot(normed_heads, out_weight, preferred_element_type=jnp.float32)
    head_count = lax.axis_size("head")
    blocks = partial_value.astype(jnp.bfloat16).reshape(length, head_count, -1)
    blocks = lax.all_to_all(
        jnp.transpose(blocks, (1, 0, 2)), "head", split_axis=0, concat_axis=0, tiled=True
    )
    attended = jnp.sum(blocks.astype(jnp.float32), axis=0)
    hidden = tokens_in.astype(jnp.float32) + attended
    steer_onehot = (steer_index[:, None] == jnp.arange(steer_table.shape[0])[None, :]).astype(
        jnp.float32
    )
    steered = hidden + jnp.dot(
        steer_onehot, steer_table, precision=EXACT_ARITHMETIC, preferred_element_type=jnp.float32
    )
    row_sums = jnp.stack([jnp.sum(hidden * hidden, axis=1), jnp.sum(steered * steered, axis=1)])
    row_sums = lax.all_to_all(
        jnp.broadcast_to(row_sums[None], (head_count,) + row_sums.shape),
        "head",
        split_axis=0,
        concat_axis=0,
        tiled=True,
    )
    sum_hidden, sum_steered = jnp.sum(row_sums, axis=0)
    rescaled = steered * jnp.sqrt((sum_hidden / D + EPS) / (sum_steered / D + EPS))[:, None]
    normed = (post_norm_weight * steered * lax.rsqrt(sum_steered / D + EPS)[:, None]).astype(
        jnp.bfloat16
    )
    experts_here = w_gate_up.shape[0]
    seq_size = lax.axis_size("seq")
    experts = experts_here * seq_size
    top_count = route_ids.shape[1]
    capacity = 5 * length * top_count // (4 * experts)
    slot_count = seq_size * capacity * experts_here
    flat_ids = route_ids.reshape(-1)
    expert_hits = (flat_ids[:, None] == jnp.arange(experts, dtype=jnp.int32)[None, :]).astype(
        jnp.int32
    )
    slot_rank = jnp.sum(jnp.cumsum(expert_hits, axis=0) * expert_hits, axis=1) - 1
    owner_dev = flat_ids // experts_here
    local_expert = flat_ids % experts_here
    slot_place = (owner_dev * capacity + slot_rank) * experts_here + local_expert
    source = (
        jnp.full((slot_count,), length, jnp.int32)
        .at[slot_place]
        .set(jnp.arange(flat_ids.shape[0], dtype=jnp.int32) // top_count)
    )
    padded_rows = jnp.concatenate([normed, jnp.zeros((1, normed.shape[1]), jnp.bfloat16)], axis=0)
    outgoing = jnp.take(padded_rows, source, axis=0).reshape(seq_size, capacity, experts_here, -1)
    arrived = lax.all_to_all(outgoing, "seq", split_axis=0, concat_axis=0, tiled=True)
    row_count = seq_size * capacity
    arrived = arrived.reshape(row_count, experts_here, -1)
    ffn_width = w_down.shape[1]
    term_rows = jnp.einsum("red,edf->ref", arrived, w_gate_up, preferred_element_type=jnp.float32)
    head_count = lax.axis_size("head")
    slice_width = ffn_width // head_count
    pieces = term_rows.astype(jnp.bfloat16).reshape(
        row_count, experts_here, 2, head_count, slice_width
    )
    pieces = lax.all_to_all(
        jnp.transpose(pieces, (3, 0, 1, 2, 4)), "head", split_axis=0, concat_axis=0, tiled=True
    )
    gate_up_slice = jnp.sum(pieces.astype(jnp.float32), axis=0)
    activated_slice = (jax.nn.silu(gate_up_slice[:, :, 0]) * gate_up_slice[:, :, 1]).astype(
        jnp.bfloat16
    )
    activated = lax.all_to_all(
        jnp.broadcast_to(activated_slice[None], (head_count,) + activated_slice.shape),
        "head",
        split_axis=0,
        concat_axis=0,
        tiled=True,
    )
    activated = jnp.transpose(activated, (1, 2, 0, 3)).reshape(row_count, experts_here, ffn_width)
    results = jnp.einsum(
        "ref,efd->red", activated, w_down, preferred_element_type=jnp.float32
    ).astype(jnp.bfloat16)
    returned = lax.all_to_all(
        results.reshape(seq_size, capacity, experts_here, -1),
        "seq",
        split_axis=0,
        concat_axis=0,
        tiled=True,
    )
    returned = returned.reshape(slot_count, -1)
    route_mix = route_weight / jnp.sum(route_weight, axis=1, keepdims=True)
    picked = jnp.take(returned, slot_place, axis=0).reshape(length, top_count, -1)
    expert_mix = jnp.sum(picked.astype(jnp.float32) * route_mix[:, :, None], axis=1)
    return (rescaled + expert_mix).astype(jnp.bfloat16)


def solution(mesh):
    placed = (
        P("seq", "head"),
        P("seq", "head"),
        P(None, "head"),
        P(None, "head"),
        P("seq", "head"),
        P("head", "seq"),
        P("head", "seq"),
        P("head", None, None),
        P(),
        P("head", None),
        P(None, "head"),
        P("seq"),
        P("head"),
        P("seq", None),
        P("seq", None),
        P("seq", "head", None),
        P("seq", None, "head"),
    )
    return jax.shard_map(
        local, mesh=mesh, in_specs=placed, out_specs=P("seq", "head"), check_vma=False
    )
```

```python
import functools

import jax
import jax.numpy as jnp
from jax import lax
from jax.sharding import PartitionSpec as P

D = 2048
HK = 16
VALUE_HEAD_COUNT = 32
DK = 128
DV = 128
KCONV = 4
STRETCH = 128
LINK = jnp.bfloat16
SCAN_RADIX = 4


EPS = 1e-06
EXACT_ARITHMETIC = lax.Precision.HIGHEST


def passed_along(value, axis, steps):
    count = lax.axis_size(axis)
    first, last = (max(0, -steps), min(count, count - steps))
    return lax.ppermute(value, axis, [(source, source + steps) for source in range(first, last)])


def unit_rows(vectors):
    return vectors / jnp.sqrt(jnp.sum(vectors * vectors, axis=-1, keepdims=True) + EPS)


def unit_lower_inverse(strict_lower):
    size_all = strict_lower.shape[-1]
    positions = jnp.arange(size_all)
    inverse = jnp.broadcast_to(jnp.eye(size_all, dtype=jnp.float32), strict_lower.shape)
    size = 1
    while size < size_all:
        same_pair = positions[:, None] // (2 * size) == positions[None, :] // (2 * size)
        lower_half = ((positions[:, None] // size) % 2 == 1) & ((positions[None, :] // size) % 2 == 0)
        coupling = jnp.where(same_pair & lower_half, -strict_lower, 0.0)
        carried = jnp.einsum("hcd,hde->hce", coupling, inverse, precision=EXACT_ARITHMETIC)
        inverse = inverse + lax.optimization_barrier(
            jnp.einsum("hcd,hde->hce", inverse, carried, precision=EXACT_ARITHMETIC)
        )
        size *= 2
    return inverse


def delta_block(want_output, carry_state, block):
    query_block, key_block, value_block, beta_block, decay_block = block
    block_len = query_block.shape[1]
    cum_decay = jnp.cumsum(decay_block, axis=-1)
    positions = jnp.arange(block_len)
    lower_mask = positions[:, None] >= positions[None, :]
    strict = positions[:, None] > positions[None, :]
    decay_diff = cum_decay[:, :, None] - cum_decay[:, None, :]
    inner = jnp.where(lower_mask, jnp.exp(jnp.where(lower_mask, decay_diff, 0.0)), 0.0)
    keys_keys = jnp.einsum("hck,hdk->hcd", key_block, key_block, precision=EXACT_ARITHMETIC)
    system = jnp.eye(block_len, dtype=jnp.float32) + beta_block[:, :, None] * jnp.where(
        strict, inner * keys_keys, 0.0
    )
    growth = jnp.exp(cum_decay)
    known_part = jnp.einsum("hck,hkw->hcw", key_block, carry_state, precision=EXACT_ARITHMETIC)
    target = beta_block[:, :, None] * (value_block - growth[:, :, None] * known_part)
    update = jnp.einsum(
        "hcd,hdw->hcw", unit_lower_inverse(system - jnp.eye(block_len, dtype=jnp.float32)),
        target, precision=EXACT_ARITHMETIC,
    )
    tail_decay = jnp.exp(cum_decay[:, -1:] - cum_decay)
    new_state = growth[:, -1][:, None, None] * carry_state + jnp.einsum(
        "hck,hcw->hkw", key_block * tail_decay[:, :, None], update, precision=EXACT_ARITHMETIC
    )
    if not want_output:
        return (new_state, None)
    query_keys = jnp.einsum("hck,hdk->hcd", query_block, key_block, precision=EXACT_ARITHMETIC)
    output = growth[:, :, None] * jnp.einsum(
        "hck,hkw->hcw", query_block, carry_state, precision=EXACT_ARITHMETIC
    )
    output = output + jnp.einsum(
        "hcd,hdw->hcw", inner * query_keys, update, precision=EXACT_ARITHMETIC
    )
    return (new_state, output)


def delta_pass(queries, key_rows, values, beta_rate, decays, state_start, want_output):
    value_heads, length = beta_rate.shape
    block_count = length // STRETCH

    def to_blocks(tensor):
        shaped = tensor.reshape((value_heads, block_count, STRETCH) + tensor.shape[2:])
        return jnp.moveaxis(shaped, 1, 0)

    state_end, outputs = lax.scan(
        functools.partial(delta_block, want_output),
        state_start,
        (
            to_blocks(queries),
            to_blocks(key_rows),
            to_blocks(values),
            to_blocks(beta_rate),
            to_blocks(decays),
        ),
    )
    if want_output:
        outputs = jnp.moveaxis(outputs, 0, 1).reshape(value_heads, length, -1)
    return (state_end, outputs)


def compose(later, earlier):
    joined = jnp.einsum("...ij,...jk->...ik", later[..., :DK], earlier, precision=EXACT_ARITHMETIC)
    return joined + jnp.concatenate([jnp.zeros_like(later[..., :DK]), later[..., DK:]], axis=-1)


def within_group(value, group, offset):
    count = lax.axis_size("seq")
    pairs = [
        (start + place, start + (place + offset) % group)
        for start in range(0, count, group)
        for place in range(group)
    ]
    return lax.ppermute(value, "seq", pairs)


def entering_state(transfer, carried, init_state):
    count, position = (lax.axis_size("seq"), lax.axis_index("seq"))
    group = transfer.shape[0]
    place = position % group
    first = position == 0
    folded = (
        jnp.einsum("hij,hjk->hik", transfer, init_state, precision=EXACT_ARITHMETIC) + carried
    )
    own = jnp.concatenate(
        [
            jnp.where(first, jnp.zeros_like(transfer), transfer),
            jnp.where(first, folded, carried),
        ],
        axis=2,
    )
    items = [lax.dynamic_index_in_dim(own, place, 0, keepdims=False)]
    for offset in range(1, group):
        sent = lax.dynamic_index_in_dim(own, (place + offset) % group, 0, keepdims=False)
        items.append(within_group(sent, group, offset))
    stacked = jnp.stack(items)
    maps = jnp.take(stacked, (place - jnp.arange(group)) % group, axis=0)
    identity = jnp.concatenate(
        [jnp.eye(DK, dtype=jnp.float32), jnp.zeros((DK, DV), jnp.float32)], axis=1
    )
    prefixes = [identity]
    for member in range(group):
        prefixes.append(compose(maps[member], prefixes[-1]) if member else maps[0])
    total = prefixes.pop()
    groups = count // group
    inclusive = total
    exclusive = None
    span = 1
    while span < groups:
        for hop in range(1, SCAN_RADIX):
            if span * hop < groups:
                part = passed_along(inclusive.astype(LINK), "seq", span * hop * group)
                part = part.astype(jnp.float32)
                exclusive = part if exclusive is None else compose(exclusive, part)
        span *= SCAN_RADIX
        if span < groups:
            inclusive = compose(total, exclusive)
    start_state = jnp.where(
        position < group,
        lax.dynamic_index_in_dim(init_state, place, 0, keepdims=False),
        exclusive[:, DK:],
    )
    prefixes = jnp.stack(prefixes)
    entering = (
        jnp.einsum("pij,jk->pik", prefixes[:, :, :DK], start_state, precision=EXACT_ARITHMETIC)
        + prefixes[:, :, DK:]
    )
    heads = [lax.dynamic_index_in_dim(entering, place, 0, keepdims=False)]
    for offset in range(1, group):
        sent = lax.dynamic_index_in_dim(entering, (place + offset) % group, 0, keepdims=False)
        heads.append(within_group(sent, group, offset))
    stacked = jnp.stack(heads)
    return jnp.take(stacked, (place - jnp.arange(group)) % group, axis=0)


def local(
    tokens_in,
    mixed_qkv,
    conv_weight,
    conv_cache,
    gate_z,
    beta_logit,
    log_decay,
    init_state,
    norm_weight,
    out_weight,
    steer_table,
    steer_index,
    post_norm_weight,
    route_ids,
    route_weight,
    w_gate_up,
    w_down,
):
    length, channels = mixed_qkv.shape
    value_heads = beta_logit.shape[0]
    group_width = 2 * DK + VALUE_HEAD_COUNT // HK * DV
    key_heads = channels // group_width
    group_size = value_heads // key_heads
    boundary_rows = passed_along(mixed_qkv[length - (KCONV - 1) :], "seq", 1)
    is_first = (lax.axis_index("seq") == 0).astype(jnp.float32)
    preceding = boundary_rows.astype(jnp.float32) + is_first * conv_cache.astype(jnp.float32)
    padded = jnp.concatenate([preceding, mixed_qkv.astype(jnp.float32)], axis=0)
    conv_taps = conv_weight.astype(jnp.float32)
    convolved = conv_taps[0] * padded[0:length]
    for offset in range(1, KCONV):
        convolved = convolved + conv_taps[offset] * padded[offset : offset + length]
    convolved = jax.nn.silu(convolved).reshape(length, key_heads, group_width)
    queries = jnp.repeat(unit_rows(convolved[:, :, :DK]) * DK ** (-0.5), group_size, axis=1)
    key_rows = jnp.repeat(unit_rows(convolved[:, :, DK : 2 * DK]), group_size, axis=1)
    values = convolved[:, :, 2 * DK :].reshape(length, value_heads, DV)
    queries = jnp.transpose(queries, (1, 0, 2))
    key_rows = jnp.transpose(key_rows, (1, 0, 2))
    values = jnp.transpose(values, (1, 0, 2))
    beta_rate = jax.nn.sigmoid(beta_logit)
    identity_maps = jnp.broadcast_to(jnp.eye(DK, dtype=jnp.float32), (value_heads, DK, DK))
    state_start = jnp.concatenate(
        [jnp.zeros((value_heads, DK, DV), jnp.float32), identity_maps], axis=2
    )
    wide_values = jnp.concatenate(
        [values, jnp.zeros((value_heads, length, DK), jnp.float32)], axis=2
    )
    state_end, wide_out = delta_pass(
        queries, key_rows, wide_values, beta_rate, log_decay, state_start, True
    )
    entering = entering_state(state_end[:, :, DV:], state_end[:, :, :DV], init_state)
    delta_out = wide_out[:, :, :DV] + jnp.einsum(
        "hlk,hkv->hlv", wide_out[:, :, DV:], entering, precision=EXACT_ARITHMETIC
    )
    delta_out = jnp.transpose(delta_out, (1, 0, 2))
    inv_rms = lax.rsqrt(jnp.mean(delta_out * delta_out, axis=-1, keepdims=True) + EPS)
    gate_act = jax.nn.silu(gate_z.astype(jnp.float32)).reshape(length, value_heads, DV)
    normed_heads = (
        (delta_out * inv_rms * norm_weight * gate_act)
        .astype(jnp.bfloat16)
        .reshape(length, value_heads * DV)
    )
    partial_value = jnp.dot(normed_heads, out_weight, preferred_element_type=jnp.float32)
    head_count = lax.axis_size("head")
    blocks = partial_value.astype(jnp.bfloat16).reshape(length, head_count, -1)
    blocks = lax.all_to_all(
        jnp.transpose(blocks, (1, 0, 2)), "head", split_axis=0, concat_axis=0, tiled=True
    )
    attended = jnp.sum(blocks.astype(jnp.float32), axis=0)
    hidden = tokens_in.astype(jnp.float32) + attended
    steer_onehot = (steer_index[:, None] == jnp.arange(steer_table.shape[0])[None, :]).astype(
        jnp.float32
    )
    steered = hidden + jnp.dot(
        steer_onehot, steer_table, precision=EXACT_ARITHMETIC, preferred_element_type=jnp.float32
    )
    row_sums = jnp.stack([jnp.sum(hidden * hidden, axis=1), jnp.sum(steered * steered, axis=1)])
    row_sums = lax.all_to_all(
        jnp.broadcast_to(row_sums[None], (head_count,) + row_sums.shape),
        "head",
        split_axis=0,
        concat_axis=0,
        tiled=True,
    )
    sum_hidden, sum_steered = jnp.sum(row_sums, axis=0)
    rescaled = steered * jnp.sqrt((sum_hidden / D + EPS) / (sum_steered / D + EPS))[:, None]
    normed = (post_norm_weight * steered * lax.rsqrt(sum_steered / D + EPS)[:, None]).astype(
        jnp.bfloat16
    )
    experts_here = w_gate_up.shape[0]
    seq_size = lax.axis_size("seq")
    experts = experts_here * seq_size
    top_count = route_ids.shape[1]
    capacity = 5 * length * top_count // (4 * experts)
    slot_count = seq_size * capacity * experts_here
    flat_ids = route_ids.reshape(-1)
    expert_hits = (flat_ids[:, None] == jnp.arange(experts, dtype=jnp.int32)[None, :]).astype(
        jnp.int32
    )
    slot_rank = jnp.sum(jnp.cumsum(expert_hits, axis=0) * expert_hits, axis=1) - 1
    owner_dev = flat_ids // experts_here
    local_expert = flat_ids % experts_here
    slot_place = (owner_dev * capacity + slot_rank) * experts_here + local_expert
    source = (
        jnp.full((slot_count,), length, jnp.int32)
        .at[slot_place]
        .set(jnp.arange(flat_ids.shape[0], dtype=jnp.int32) // top_count)
    )
    padded_rows = jnp.concatenate([normed, jnp.zeros((1, normed.shape[1]), jnp.bfloat16)], axis=0)
    outgoing = jnp.take(padded_rows, source, axis=0).reshape(seq_size, capacity, experts_here, -1)
    arrived = lax.all_to_all(outgoing, "seq", split_axis=0, concat_axis=0, tiled=True)
    row_count = seq_size * capacity
    arrived = arrived.reshape(row_count, experts_here, -1)
    ffn_width = w_down.shape[1]
    term_rows = jnp.einsum("red,edf->ref", arrived, w_gate_up, preferred_element_type=jnp.float32)
    head_count = lax.axis_size("head")
    slice_width = ffn_width // head_count
    pieces = term_rows.astype(jnp.bfloat16).reshape(
        row_count, experts_here, 2, head_count, slice_width
    )
    pieces = lax.all_to_all(
        jnp.transpose(pieces, (3, 0, 1, 2, 4)), "head", split_axis=0, concat_axis=0, tiled=True
    )
    gate_up_slice = jnp.sum(pieces.astype(jnp.float32), axis=0)
    activated_slice = (jax.nn.silu(gate_up_slice[:, :, 0]) * gate_up_slice[:, :, 1]).astype(
        jnp.bfloat16
    )
    activated = lax.all_to_all(
        jnp.broadcast_to(activated_slice[None], (head_count,) + activated_slice.shape),
        "head",
        split_axis=0,
        concat_axis=0,
        tiled=True,
    )
    activated = jnp.transpose(activated, (1, 2, 0, 3)).reshape(row_count, experts_here, ffn_width)
    results = jnp.einsum(
        "ref,efd->red", activated, w_down, preferred_element_type=jnp.float32
    ).astype(jnp.bfloat16)
    returned = lax.all_to_all(
        results.reshape(seq_size, capacity, experts_here, -1),
        "seq",
        split_axis=0,
        concat_axis=0,
        tiled=True,
    )
    returned = returned.reshape(slot_count, -1)
    route_mix = route_weight / jnp.sum(route_weight, axis=1, keepdims=True)
    picked = jnp.take(returned, slot_place, axis=0).reshape(length, top_count, -1)
    expert_mix = jnp.sum(picked.astype(jnp.float32) * route_mix[:, :, None], axis=1)
    return (rescaled + expert_mix).astype(jnp.bfloat16)


def solution(mesh):
    placed = (
        P("seq", "head"),
        P("seq", "head"),
        P(None, "head"),
        P(None, "head"),
        P("seq", "head"),
        P("head", "seq"),
        P("head", "seq"),
        P("head", None, None),
        P(),
        P("head", None),
        P(None, "head"),
        P("seq"),
        P("head"),
        P("seq", None),
        P("seq", None),
        P("seq", "head", None),
        P("seq", None, "head"),
    )
    return jax.shard_map(
        local, mesh=mesh, in_specs=placed, out_specs=P("seq", "head"), check_vma=False
    )
```

```python
import functools

import jax
import jax.numpy as jnp
from jax import lax
from jax.sharding import PartitionSpec as P

D = 2048
HK = 16
VALUE_HEAD_COUNT = 32
DK = 128
DV = 128
KCONV = 4
STRETCH = 128
LINK = jnp.bfloat16
SCAN_RADIX = 4


EPS = 1e-06
EXACT_ARITHMETIC = lax.Precision.HIGHEST


def passed_along(value, axis, steps):
    count = lax.axis_size(axis)
    first, last = (max(0, -steps), min(count, count - steps))
    return lax.ppermute(value, axis, [(source, source + steps) for source in range(first, last)])


def unit_rows(vectors):
    return vectors / jnp.sqrt(jnp.sum(vectors * vectors, axis=-1, keepdims=True) + EPS)


def unit_lower_inverse(strict_lower):
    size_all = strict_lower.shape[-1]
    positions = jnp.arange(size_all)
    inverse = jnp.broadcast_to(jnp.eye(size_all, dtype=jnp.float32), strict_lower.shape)
    size = 1
    while size < size_all:
        same_pair = positions[:, None] // (2 * size) == positions[None, :] // (2 * size)
        lower_half = ((positions[:, None] // size) % 2 == 1) & ((positions[None, :] // size) % 2 == 0)
        coupling = jnp.where(same_pair & lower_half, -strict_lower, 0.0)
        carried = jnp.einsum("hcd,hde->hce", coupling, inverse, precision=EXACT_ARITHMETIC)
        inverse = inverse + lax.optimization_barrier(
            jnp.einsum("hcd,hde->hce", inverse, carried, precision=EXACT_ARITHMETIC)
        )
        size *= 2
    return inverse


def delta_block(want_output, carry_state, block):
    query_block, key_block, value_block, beta_block, decay_block = block
    block_len = query_block.shape[1]
    cum_decay = jnp.cumsum(decay_block, axis=-1)
    positions = jnp.arange(block_len)
    lower_mask = positions[:, None] >= positions[None, :]
    strict = positions[:, None] > positions[None, :]
    decay_diff = cum_decay[:, :, None] - cum_decay[:, None, :]
    inner = jnp.where(lower_mask, jnp.exp(jnp.where(lower_mask, decay_diff, 0.0)), 0.0)
    keys_keys = jnp.einsum("hck,hdk->hcd", key_block, key_block, precision=EXACT_ARITHMETIC)
    system = jnp.eye(block_len, dtype=jnp.float32) + beta_block[:, :, None] * jnp.where(
        strict, inner * keys_keys, 0.0
    )
    growth = jnp.exp(cum_decay)
    known_part = jnp.einsum("hck,hkw->hcw", key_block, carry_state, precision=EXACT_ARITHMETIC)
    target = beta_block[:, :, None] * (value_block - growth[:, :, None] * known_part)
    update = jnp.einsum(
        "hcd,hdw->hcw", unit_lower_inverse(system - jnp.eye(block_len, dtype=jnp.float32)),
        target, precision=EXACT_ARITHMETIC,
    )
    tail_decay = jnp.exp(cum_decay[:, -1:] - cum_decay)
    new_state = growth[:, -1][:, None, None] * carry_state + jnp.einsum(
        "hck,hcw->hkw", key_block * tail_decay[:, :, None], update, precision=EXACT_ARITHMETIC
    )
    if not want_output:
        return (new_state, None)
    query_keys = jnp.einsum("hck,hdk->hcd", query_block, key_block, precision=EXACT_ARITHMETIC)
    output = growth[:, :, None] * jnp.einsum(
        "hck,hkw->hcw", query_block, carry_state, precision=EXACT_ARITHMETIC
    )
    output = output + jnp.einsum(
        "hcd,hdw->hcw", inner * query_keys, update, precision=EXACT_ARITHMETIC
    )
    return (new_state, output)


def delta_pass(queries, key_rows, values, beta_rate, decays, state_start, want_output):
    value_heads, length = beta_rate.shape
    block_count = length // STRETCH

    def to_blocks(tensor):
        shaped = tensor.reshape((value_heads, block_count, STRETCH) + tensor.shape[2:])
        return jnp.moveaxis(shaped, 1, 0)

    state_end, outputs = lax.scan(
        functools.partial(delta_block, want_output),
        state_start,
        (
            to_blocks(queries),
            to_blocks(key_rows),
            to_blocks(values),
            to_blocks(beta_rate),
            to_blocks(decays),
        ),
    )
    if want_output:
        outputs = jnp.moveaxis(outputs, 0, 1).reshape(value_heads, length, -1)
    return (state_end, outputs)


def compose(later, earlier):
    joined = jnp.einsum("...ij,...jk->...ik", later[..., :DK], earlier, precision=EXACT_ARITHMETIC)
    return joined + jnp.concatenate([jnp.zeros_like(later[..., :DK]), later[..., DK:]], axis=-1)


def within_group(value, group, offset):
    count = lax.axis_size("seq")
    pairs = [
        (start + place, start + (place + offset) % group)
        for start in range(0, count, group)
        for place in range(group)
    ]
    return lax.ppermute(value, "seq", pairs)


def entering_state(transfer, carried, init_state):
    count, position = (lax.axis_size("seq"), lax.axis_index("seq"))
    group = transfer.shape[0]
    place = position % group
    first = position == 0
    folded = (
        jnp.einsum("hij,hjk->hik", transfer, init_state, precision=EXACT_ARITHMETIC) + carried
    )
    own = jnp.concatenate(
        [
            jnp.where(first, jnp.zeros_like(transfer), transfer),
            jnp.where(first, folded, carried),
        ],
        axis=2,
    )
    items = [lax.dynamic_index_in_dim(own, place, 0, keepdims=False)]
    for offset in range(1, group):
        sent = lax.dynamic_index_in_dim(own, (place + offset) % group, 0, keepdims=False)
        items.append(within_group(sent.astype(LINK), group, offset).astype(jnp.float32))
    stacked = jnp.stack(items)
    maps = jnp.take(stacked, (place - jnp.arange(group)) % group, axis=0)
    identity = jnp.concatenate(
        [jnp.eye(DK, dtype=jnp.float32), jnp.zeros((DK, DV), jnp.float32)], axis=1
    )
    prefixes = [identity]
    for member in range(group):
        prefixes.append(compose(maps[member], prefixes[-1]) if member else maps[0])
    total = prefixes.pop()
    groups = count // group
    inclusive = total
    exclusive = None
    span = 1
    while span < groups:
        for hop in range(1, SCAN_RADIX):
            if span * hop < groups:
                part = passed_along(inclusive.astype(LINK), "seq", span * hop * group)
                part = part.astype(jnp.float32)
                exclusive = part if exclusive is None else compose(exclusive, part)
        span *= SCAN_RADIX
        if span < groups:
            inclusive = compose(total, exclusive)
    start_state = jnp.where(
        position < group,
        lax.dynamic_index_in_dim(init_state, place, 0, keepdims=False),
        exclusive[:, DK:],
    )
    prefixes = jnp.stack(prefixes)
    entering = (
        jnp.einsum("pij,jk->pik", prefixes[:, :, :DK], start_state, precision=EXACT_ARITHMETIC)
        + prefixes[:, :, DK:]
    )
    heads = [lax.dynamic_index_in_dim(entering, place, 0, keepdims=False)]
    for offset in range(1, group):
        sent = lax.dynamic_index_in_dim(entering, (place + offset) % group, 0, keepdims=False)
        heads.append(within_group(sent.astype(LINK), group, offset).astype(jnp.float32))
    stacked = jnp.stack(heads)
    return jnp.take(stacked, (place - jnp.arange(group)) % group, axis=0)


def local(
    tokens_in,
    mixed_qkv,
    conv_weight,
    conv_cache,
    gate_z,
    beta_logit,
    log_decay,
    init_state,
    norm_weight,
    out_weight,
    steer_table,
    steer_index,
    post_norm_weight,
    route_ids,
    route_weight,
    w_gate_up,
    w_down,
):
    length, channels = mixed_qkv.shape
    value_heads = beta_logit.shape[0]
    group_width = 2 * DK + VALUE_HEAD_COUNT // HK * DV
    key_heads = channels // group_width
    group_size = value_heads // key_heads
    boundary_rows = passed_along(mixed_qkv[length - (KCONV - 1) :], "seq", 1)
    is_first = (lax.axis_index("seq") == 0).astype(jnp.float32)
    preceding = boundary_rows.astype(jnp.float32) + is_first * conv_cache.astype(jnp.float32)
    padded = jnp.concatenate([preceding, mixed_qkv.astype(jnp.float32)], axis=0)
    conv_taps = conv_weight.astype(jnp.float32)
    convolved = conv_taps[0] * padded[0:length]
    for offset in range(1, KCONV):
        convolved = convolved + conv_taps[offset] * padded[offset : offset + length]
    convolved = jax.nn.silu(convolved).reshape(length, key_heads, group_width)
    queries = jnp.repeat(unit_rows(convolved[:, :, :DK]) * DK ** (-0.5), group_size, axis=1)
    key_rows = jnp.repeat(unit_rows(convolved[:, :, DK : 2 * DK]), group_size, axis=1)
    values = convolved[:, :, 2 * DK :].reshape(length, value_heads, DV)
    queries = jnp.transpose(queries, (1, 0, 2))
    key_rows = jnp.transpose(key_rows, (1, 0, 2))
    values = jnp.transpose(values, (1, 0, 2))
    beta_rate = jax.nn.sigmoid(beta_logit)
    identity_maps = jnp.broadcast_to(jnp.eye(DK, dtype=jnp.float32), (value_heads, DK, DK))
    state_start = jnp.concatenate(
        [jnp.zeros((value_heads, DK, DV), jnp.float32), identity_maps], axis=2
    )
    wide_values = jnp.concatenate(
        [values, jnp.zeros((value_heads, length, DK), jnp.float32)], axis=2
    )
    state_end, wide_out = delta_pass(
        queries, key_rows, wide_values, beta_rate, log_decay, state_start, True
    )
    entering = entering_state(state_end[:, :, DV:], state_end[:, :, :DV], init_state)
    delta_out = wide_out[:, :, :DV] + jnp.einsum(
        "hlk,hkv->hlv", wide_out[:, :, DV:], entering, precision=EXACT_ARITHMETIC
    )
    delta_out = jnp.transpose(delta_out, (1, 0, 2))
    inv_rms = lax.rsqrt(jnp.mean(delta_out * delta_out, axis=-1, keepdims=True) + EPS)
    gate_act = jax.nn.silu(gate_z.astype(jnp.float32)).reshape(length, value_heads, DV)
    normed_heads = (
        (delta_out * inv_rms * norm_weight * gate_act)
        .astype(jnp.bfloat16)
        .reshape(length, value_heads * DV)
    )
    partial_value = jnp.dot(normed_heads, out_weight, preferred_element_type=jnp.float32)
    head_count = lax.axis_size("head")
    blocks = partial_value.astype(jnp.bfloat16).reshape(length, head_count, -1)
    blocks = lax.all_to_all(
        jnp.transpose(blocks, (1, 0, 2)), "head", split_axis=0, concat_axis=0, tiled=True
    )
    attended = jnp.sum(blocks.astype(jnp.float32), axis=0)
    hidden = tokens_in.astype(jnp.float32) + attended
    steer_onehot = (steer_index[:, None] == jnp.arange(steer_table.shape[0])[None, :]).astype(
        jnp.float32
    )
    steered = hidden + jnp.dot(
        steer_onehot, steer_table, precision=EXACT_ARITHMETIC, preferred_element_type=jnp.float32
    )
    row_sums = jnp.stack([jnp.sum(hidden * hidden, axis=1), jnp.sum(steered * steered, axis=1)])
    row_sums = lax.all_to_all(
        jnp.broadcast_to(row_sums[None], (head_count,) + row_sums.shape),
        "head",
        split_axis=0,
        concat_axis=0,
        tiled=True,
    )
    sum_hidden, sum_steered = jnp.sum(row_sums, axis=0)
    rescaled = steered * jnp.sqrt((sum_hidden / D + EPS) / (sum_steered / D + EPS))[:, None]
    normed = (post_norm_weight * steered * lax.rsqrt(sum_steered / D + EPS)[:, None]).astype(
        jnp.bfloat16
    )
    experts_here = w_gate_up.shape[0]
    seq_size = lax.axis_size("seq")
    experts = experts_here * seq_size
    top_count = route_ids.shape[1]
    capacity = 5 * length * top_count // (4 * experts)
    slot_count = seq_size * capacity * experts_here
    flat_ids = route_ids.reshape(-1)
    expert_hits = (flat_ids[:, None] == jnp.arange(experts, dtype=jnp.int32)[None, :]).astype(
        jnp.int32
    )
    slot_rank = jnp.sum(jnp.cumsum(expert_hits, axis=0) * expert_hits, axis=1) - 1
    owner_dev = flat_ids // experts_here
    local_expert = flat_ids % experts_here
    slot_place = (owner_dev * capacity + slot_rank) * experts_here + local_expert
    source = (
        jnp.full((slot_count,), length, jnp.int32)
        .at[slot_place]
        .set(jnp.arange(flat_ids.shape[0], dtype=jnp.int32) // top_count)
    )
    padded_rows = jnp.concatenate([normed, jnp.zeros((1, normed.shape[1]), jnp.bfloat16)], axis=0)
    outgoing = jnp.take(padded_rows, source, axis=0).reshape(seq_size, capacity, experts_here, -1)
    arrived = lax.all_to_all(outgoing, "seq", split_axis=0, concat_axis=0, tiled=True)
    row_count = seq_size * capacity
    arrived = arrived.reshape(row_count, experts_here, -1)
    ffn_width = w_down.shape[1]
    term_rows = jnp.einsum("red,edf->ref", arrived, w_gate_up, preferred_element_type=jnp.float32)
    head_count = lax.axis_size("head")
    slice_width = ffn_width // head_count
    pieces = term_rows.astype(jnp.bfloat16).reshape(
        row_count, experts_here, 2, head_count, slice_width
    )
    pieces = lax.all_to_all(
        jnp.transpose(pieces, (3, 0, 1, 2, 4)), "head", split_axis=0, concat_axis=0, tiled=True
    )
    gate_up_slice = jnp.sum(pieces.astype(jnp.float32), axis=0)
    activated_slice = (jax.nn.silu(gate_up_slice[:, :, 0]) * gate_up_slice[:, :, 1]).astype(
        jnp.bfloat16
    )
    activated = lax.all_to_all(
        jnp.broadcast_to(activated_slice[None], (head_count,) + activated_slice.shape),
        "head",
        split_axis=0,
        concat_axis=0,
        tiled=True,
    )
    activated = jnp.transpose(activated, (1, 2, 0, 3)).reshape(row_count, experts_here, ffn_width)
    results = jnp.einsum(
        "ref,efd->red", activated, w_down, preferred_element_type=jnp.float32
    ).astype(jnp.bfloat16)
    returned = lax.all_to_all(
        results.reshape(seq_size, capacity, experts_here, -1),
        "seq",
        split_axis=0,
        concat_axis=0,
        tiled=True,
    )
    returned = returned.reshape(slot_count, -1)
    route_mix = route_weight / jnp.sum(route_weight, axis=1, keepdims=True)
    picked = jnp.take(returned, slot_place, axis=0).reshape(length, top_count, -1)
    expert_mix = jnp.sum(picked.astype(jnp.float32) * route_mix[:, :, None], axis=1)
    return (rescaled + expert_mix).astype(jnp.bfloat16)


def solution(mesh):
    placed = (
        P("seq", "head"),
        P("seq", "head"),
        P(None, "head"),
        P(None, "head"),
        P("seq", "head"),
        P("head", "seq"),
        P("head", "seq"),
        P("head", None, None),
        P(),
        P("head", None),
        P(None, "head"),
        P("seq"),
        P("head"),
        P("seq", None),
        P("seq", None),
        P("seq", "head", None),
        P("seq", None, "head"),
    )
    return jax.shard_map(
        local, mesh=mesh, in_specs=placed, out_specs=P("seq", "head"), check_vma=False
    )
```
